32 devices in a mesh: energy: 8 (over z, x), dom: 4 (over y, core).
Axes of the slice: x: 2, y: 2, z: 4, core: 2. Of those that a mesh axis runs over, the one named last changes fastest.
Arguments:
- hamiltonian: float32 [4, 256, 256], P('dom'), may hold values from -0.005 to 2.4, as said below
- coupling: float32 [4, 256, 256], P('dom'), may hold values from -0.0025 to 1.05
- deform: float32 [4, 256], P('dom'), may hold values from 0.4 to 1
- green_prev: bfloat16 [8, 4, 2, 256, 256], P('energy', 'dom'), may hold values from -0.78 to 0.78
- energy_grid: float32 [8], replicated, may hold values from -0.03 to 0.03
- slot_energy: int32 [8], replicated, may hold values from 0 to 7, each once
- phonon_offsets: int32 [2, 8], replicated, may hold values from 1 to 3
Outputs:
- green_new: float32 [8, 4, 2, 256, 256], P('energy', 'dom')
The draws below stay inside these ranges and needn't reach their ends.
Inputs may be any that keep to these rules, and one draw needn't show every extreme that they name: `slot_energy`: each energy point stands in exactly one slot. `hamiltonian`: each block is symmetric.
All inputs are finite; a program needn't handle non-finite values.
Results may differ from the reference program's by a relative error of at most 0.0003.
Values may be sent and summed in bfloat16 or wider, within the bound.
No kernel may reach another device: no remote copies, remote signals or barrier semaphores. Data moves between devices by JAX's collectives and lax.ppermute only.
A program may use at most 64 MiB of HBM per device.

```python
import math
import jax
import jax.numpy as jnp
from jax import lax

B = 256
BW = 32
NSLAB = 4
NE = 8


def edge_fields(key):
    key_link, key_gap = jax.random.split(jax.random.fold_in(key, 31))
    link_diag = jax.random.uniform(key_link, (NSLAB, B), jnp.float32, 0.95, 1.05)
    gap_unit = jax.random.uniform(key_gap, (NSLAB, B), jnp.float32, 0.0, 1.0)
    return (link_diag, gap_unit)


def draw_hamiltonian(key, part):
    link_diag, gap_unit = edge_fields(key)
    key_off = jax.random.fold_in(key, 11)
    spread = 0.015 / math.sqrt(B)
    gap = jnp.exp(math.log(0.06) + gap_unit * (math.log(0.3) - math.log(0.06)))
    noise = jax.random.normal(key_off, (NSLAB, B, B), jnp.float32) * spread
    noise = (noise + jnp.swapaxes(noise, 1, 2)) * 0.70710678
    noise = jnp.clip(noise, -0.005, 0.005)
    previous_link = jnp.concatenate([link_diag[:1], link_diag[:-1]], axis=0)
    diagonal = previous_link + link_diag + gap
    eye_mat = jnp.eye(B, dtype=jnp.float32)
    return noise * (1.0 - eye_mat) + diagonal[:, :, None] * eye_mat


def draw_coupling(key, part):
    link_diag, gap_unit = edge_fields(key)
    key_off = jax.random.fold_in(key, 23)
    spread = 0.01 / math.sqrt(B)
    noise = jax.random.normal(key_off, (NSLAB, B, B), jnp.float32) * spread
    noise = jnp.clip(noise, -0.0025, 0.0025)
    eye_mat = jnp.eye(B, dtype=jnp.float32)
    return noise * (1.0 - eye_mat) + link_diag[:, :, None] * eye_mat


def draw_green_prev(key, part):
    key_real, key_imag = jax.random.split(jax.random.fold_in(key, 47))
    positions = jnp.arange(B).astype(jnp.float32)
    distance = jnp.abs(positions[:, None] - positions[None, :])
    envelope = jnp.exp(-distance / (0.5 * BW))
    block_shape = (NE, NSLAB, B, B)
    amplitude = 0.45
    factor_real = jnp.clip(1.0 + 0.2 * jax.random.normal(key_real, block_shape, jnp.float32), 0.6, 1.4)
    factor_imag = jnp.clip(1.0 + 0.2 * jax.random.normal(key_imag, block_shape, jnp.float32), 0.6, 1.4)
    real_part = amplitude * envelope * factor_real
    imag_part = -amplitude * envelope * factor_imag
    return jnp.clip(jnp.stack([real_part, imag_part], axis=2), -0.765, 0.765).astype(jnp.bfloat16)


def with_ends(entries, own_key, least, top_value):
    longest = entries.shape.index(max(entries.shape))
    spots = []
    for shift in (0, 1):
        where = [jax.random.randint(jax.random.fold_in(own_key, axis), (), 0, length) for axis, length in enumerate(entries.shape)]
        where[longest] = (where[longest] + shift) % entries.shape[longest]
        spots.append(tuple(where))
    return entries.at[spots[0]].set(least).at[spots[1]].set(top_value)


def block_levels(rng, shape, cuts, least, high):
    loudness = 1.0
    for axis_at, parts in cuts:
        draws = jax.random.uniform(jax.random.fold_in(jax.random.fold_in(rng, 6), axis_at), (parts,), jnp.float32, least / len(cuts), high / len(cuts))
        loudness = loudness * jnp.repeat(jnp.exp(draws), shape[axis_at] // parts).reshape((-1,) + (1,) * (len(shape) - 1 - axis_at))
    return loudness


def setup_inputs(seed: int = 0) -> dict:
    key_list = jax.random.split(jax.random.key(seed), 8)
    return {
        "hamiltonian": draw_hamiltonian(jax.random.fold_in(key_list[7], 71), 0),
        "coupling": draw_coupling(jax.random.fold_in(key_list[7], 71), 0),
        "deform": jnp.clip(jnp.exp(math.log(1.0) - 0.9162907 * jax.random.uniform(key_list[2], (NSLAB, B), jnp.float32) ** block_levels(key_list[2], (NSLAB, B), ((0, 4),), -0.2, 0.2)), 0.4, 1.0),
        "green_prev": draw_green_prev(jax.random.fold_in(key_list[7], 71), 0),
        "energy_grid": jnp.clip(jax.random.uniform(key_list[4], (NE,), jnp.float32, -0.03, 0.03), -0.03, 0.03),
        "slot_energy": jax.random.permutation(key_list[5], NE).astype(jnp.int32),
        "phonon_offsets": with_ends(jax.random.randint(key_list[6], (2, NE), 1, 4), jax.random.fold_in(key_list[6], 1), 1, 3).astype(jnp.int32),
    }


emission_weight = 1.3
absorb_weight = 0.3
couple_scale = 0.04
broaden = 0.02
lead_gamma = 0.1
lead_scale = 0.1

def symmetric(matrix):
    return 0.5 * (matrix + jnp.swapaxes(matrix, -1, -2))

def invert_pair(block_re, block_im):
    orbitals = block_re.shape[-1]
    eye_mat = jnp.eye(orbitals, dtype=block_re.dtype)
    first_factor = jnp.linalg.cholesky(block_re)
    solved_ratio = jax.scipy.linalg.cho_solve((first_factor, True), block_im)
    merged = symmetric(block_re + jnp.dot(block_im, solved_ratio, precision=lax.Precision.HIGHEST))
    second_factor = jnp.linalg.cholesky(merged)
    inv_re = jax.scipy.linalg.cho_solve((second_factor, True), eye_mat)
    inv_im = jnp.dot(solved_ratio, inv_re, precision=lax.Precision.HIGHEST)
    return (inv_re, inv_im)

def forward_sweep(block_re, block_im, coupling, start_re, start_im):

    def advance(state_pair, slab_data):
        left_re, left_im = state_pair
        own_re, own_im, link_block = slab_data
        inv_re, inv_im = invert_pair(own_re + left_re, own_im + left_im)
        next_re = -symmetric(jnp.dot(link_block.T, jnp.dot(inv_re, link_block, precision=lax.Precision.HIGHEST), precision=lax.Precision.HIGHEST))
        next_im = symmetric(jnp.dot(link_block.T, jnp.dot(inv_im, link_block, precision=lax.Precision.HIGHEST), precision=lax.Precision.HIGHEST))
        return ((next_re, next_im), (left_re, left_im))
    final_pair, slab_terms = lax.scan(advance, (start_re, start_im), (block_re, block_im, coupling))
    return (slab_terms, final_pair)

def backward_sweep(block_re, block_im, coupling, start_re, start_im):

    def retreat(state_pair, slab_data):
        after_re, after_im = state_pair
        own_re, own_im, link_block = slab_data
        right_re = -symmetric(jnp.dot(link_block, jnp.dot(after_re, link_block.T, precision=lax.Precision.HIGHEST), precision=lax.Precision.HIGHEST))
        right_im = symmetric(jnp.dot(link_block, jnp.dot(after_im, link_block.T, precision=lax.Precision.HIGHEST), precision=lax.Precision.HIGHEST))
        inv_re, inv_im = invert_pair(own_re + right_re, own_im + right_im)
        return ((inv_re, inv_im), (right_re, right_im))
    final_pair, slab_terms = lax.scan(retreat, (start_re, start_im), (block_re, block_im, coupling), reverse=True)
    return (slab_terms, final_pair)

def slab_blocks(hamiltonian, coupling, deform, fetched, energy, first_mask, last_mask):
    orbitals = hamiltonian.shape[-1]
    positions = jnp.arange(orbitals)
    distance = jnp.abs(positions[:, None] - positions[None, :]).astype(hamiltonian.dtype)
    profile = jnp.where(distance <= BW, jnp.exp(-2.0 * distance / BW), 0.0).astype(hamiltonian.dtype)
    weight = couple_scale * deform[:, :, None] * deform[:, None, :] * profile
    mixed_part = symmetric(fetched)
    sigma_re = weight * mixed_part[:, 0]
    sigma_im = weight * mixed_part[:, 1]
    eye_mat = jnp.eye(orbitals, dtype=hamiltonian.dtype)
    lead_term = lead_scale * jnp.matmul(jnp.swapaxes(coupling, 1, 2), coupling, precision=lax.Precision.HIGHEST)
    block_re = hamiltonian - energy * eye_mat + sigma_re
    block_im = broaden * eye_mat - sigma_im + first_mask[:, None, None] * lead_gamma * eye_mat + last_mask[:, None, None] * lead_term
    return (block_re, block_im)

def partner_levels(energy_level, phonon_offsets, level_count):
    lower_level = energy_level - phonon_offsets[0, energy_level]
    upper_level = energy_level + phonon_offsets[1, energy_level]
    lower_level = jnp.where(lower_level >= 0, lower_level, -1).astype(jnp.int32)
    upper_level = jnp.where(upper_level < level_count, upper_level, -1).astype(jnp.int32)
    return (lower_level, upper_level)

def reference(hamiltonian, coupling, deform, green_prev, energy_grid, slot_energy, phonon_offsets):
    level_count = slot_energy.shape[0]
    slab_count = hamiltonian.shape[0]
    orbitals = hamiltonian.shape[-1]
    slot_of = jnp.zeros((level_count,), jnp.int32).at[slot_energy].set(jnp.arange(level_count, dtype=jnp.int32))
    slab_index = jnp.arange(slab_count)
    first_mask = (slab_index == 0).astype(hamiltonian.dtype)
    last_mask = (slab_index == slab_count - 1).astype(hamiltonian.dtype)
    zero_block = jnp.zeros((orbitals, orbitals), hamiltonian.dtype)

    def solve_slot(own_slot):
        energy_level = slot_energy[own_slot]
        energy = energy_grid[energy_level]
        lower_level, upper_level = partner_levels(energy_level, phonon_offsets, level_count)
        low_part = green_prev[slot_of[jnp.maximum(lower_level, 0)]].astype(hamiltonian.dtype)
        high_part = green_prev[slot_of[jnp.maximum(upper_level, 0)]].astype(hamiltonian.dtype)
        low_weight = jnp.where(lower_level >= 0, emission_weight, 0.0).astype(hamiltonian.dtype)
        high_weight = jnp.where(upper_level >= 0, absorb_weight, 0.0).astype(hamiltonian.dtype)
        fetched = low_weight * low_part + high_weight * high_part
        block_re, block_im = slab_blocks(hamiltonian, coupling, deform, fetched, energy, first_mask, last_mask)
        left_terms, unused_left = forward_sweep(block_re, block_im, coupling, zero_block, zero_block)
        right_terms, unused_right = backward_sweep(block_re, block_im, coupling, zero_block, zero_block)
        inv_re, inv_im = jax.vmap(invert_pair)(block_re + left_terms[0] + right_terms[0], block_im + left_terms[1] + right_terms[1])
        return jnp.stack([-inv_re, -inv_im], axis=1)
    return lax.map(solve_slot, jnp.arange(level_count, dtype=jnp.int32))
```

```python
import jax
import jax.numpy as jnp
from jax import lax
from jax.sharding import PartitionSpec as P

BW = 32


emission_weight = 1.3
absorb_weight = 0.3
couple_scale = 0.04
broaden = 0.02
lead_gamma = 0.1
lead_scale = 0.1

HI = lax.Precision.HIGHEST


def symmetric(matrix):
    return 0.5 * (matrix + jnp.swapaxes(matrix, -1, -2))


def invert_pair(block_re, block_im):
    orbitals = block_re.shape[-1]
    eye_mat = jnp.eye(orbitals, dtype=block_re.dtype)
    first_factor = jnp.linalg.cholesky(block_re)
    solved_ratio = jax.scipy.linalg.cho_solve((first_factor, True), block_im)
    merged = symmetric(block_re + jnp.dot(block_im, solved_ratio, precision=HI))
    second_factor = jnp.linalg.cholesky(merged)
    inv_re = jax.scipy.linalg.cho_solve((second_factor, True), eye_mat)
    inv_im = jnp.dot(solved_ratio, inv_re, precision=HI)
    return (inv_re, inv_im)


def slab_blocks(hamiltonian, coupling, deform, fetched, energy, first_mask, last_mask):
    orbitals = hamiltonian.shape[-1]
    positions = jnp.arange(orbitals)
    distance = jnp.abs(positions[:, None] - positions[None, :]).astype(hamiltonian.dtype)
    profile = jnp.where(distance <= BW, jnp.exp(-2.0 * distance / BW), 0.0)
    weight = couple_scale * deform[:, :, None] * deform[:, None, :] * profile
    mixed_part = symmetric(fetched)
    sigma_re = weight * mixed_part[:, 0]
    sigma_im = weight * mixed_part[:, 1]
    eye_mat = jnp.eye(orbitals, dtype=hamiltonian.dtype)
    lead_term = lead_scale * jnp.matmul(jnp.swapaxes(coupling, 1, 2), coupling, precision=HI)
    block_re = hamiltonian - energy * eye_mat + sigma_re
    block_im = (
        broaden * eye_mat
        - sigma_im
        + first_mask[:, None, None] * lead_gamma * eye_mat
        + last_mask[:, None, None] * lead_term
    )
    return (block_re, block_im)


def partner_levels(energy_level, phonon_offsets, level_count):
    lower_level = energy_level - phonon_offsets[0, energy_level]
    upper_level = energy_level + phonon_offsets[1, energy_level]
    lower_level = jnp.where(lower_level >= 0, lower_level, -1)
    upper_level = jnp.where(upper_level < level_count, upper_level, -1)
    return (lower_level, upper_level)


def body(hamiltonian, coupling, deform, green_prev, energy_grid, slot_energy, phonon_offsets):
    local_slabs = hamiltonian.shape[0]
    level_count = slot_energy.shape[0]
    dom_count = lax.axis_size("dom")
    dom_index = lax.axis_index("dom")
    slab_total = local_slabs * dom_count
    own_slot = lax.axis_index("energy")
    energy_level = slot_energy[own_slot]
    energy = energy_grid[energy_level]
    lower_level, upper_level = partner_levels(energy_level, phonon_offsets, level_count)
    weights = emission_weight * (slot_energy == lower_level).astype(jnp.float32) + absorb_weight * (
        slot_energy == upper_level
    ).astype(jnp.float32)
    fetched = jnp.einsum(
        "n,nsabc->sabc",
        weights,
        lax.all_gather(green_prev, "energy", axis=0, tiled=True).astype(jnp.float32),
        precision=HI,
    )
    global_index = dom_index * local_slabs + jnp.arange(local_slabs)
    first_mask = (global_index == 0).astype(jnp.float32)
    last_mask = (global_index == slab_total - 1).astype(jnp.float32)
    block_re, block_im = slab_blocks(
        hamiltonian, coupling, deform, fetched, energy, first_mask, last_mask
    )
    gathered = lax.all_gather(
        jnp.stack([block_re, block_im, coupling]), "dom", axis=1, tiled=True
    )
    all_re, all_im, all_link = gathered[0], gathered[1], gathered[2]
    orbitals = hamiltonian.shape[-1]
    zero_block = jnp.zeros((orbitals, orbitals), jnp.float32)

    outputs = []
    for local in range(local_slabs):
        own = dom_index * local_slabs + local

        def chain_step(step, carry):
            left_re, left_im, right_re, right_im = carry
            is_left = step < own
            slab = jnp.where(is_left, step, slab_total - 1 - step + own)
            acc_re = jnp.where(is_left, left_re, right_re)
            acc_im = jnp.where(is_left, left_im, right_im)
            inv_re, inv_im = invert_pair(all_re[slab] + acc_re, all_im[slab] + acc_im)
            link_index = jnp.where(is_left, step, jnp.maximum(slab - 1, 0))
            link_block = all_link[link_index]
            link_block = jnp.where(is_left, link_block, link_block.T)
            next_re = -symmetric(
                jnp.dot(link_block.T, jnp.dot(inv_re, link_block, precision=HI), precision=HI)
            )
            next_im = symmetric(
                jnp.dot(link_block.T, jnp.dot(inv_im, link_block, precision=HI), precision=HI)
            )
            left_re = jnp.where(is_left, next_re, left_re)
            left_im = jnp.where(is_left, next_im, left_im)
            right_re = jnp.where(is_left, right_re, next_re)
            right_im = jnp.where(is_left, right_im, next_im)
            return (left_re, left_im, right_re, right_im)

        left_re, left_im, right_re, right_im = lax.fori_loop(
            0, slab_total - 1, chain_step, (zero_block, zero_block, zero_block, zero_block)
        )
        inv_re, inv_im = invert_pair(
            block_re[local] + left_re + right_re, block_im[local] + left_im + right_im
        )
        outputs.append(jnp.stack([-inv_re, -inv_im]))
    return jnp.stack(outputs)[None]


def solution(mesh):
    in_specs = (
        P("dom", None, None),
        P("dom", None, None),
        P("dom", None),
        P("energy", "dom", None, None, None),
        P(),
        P(),
        P(),
    )
    out_specs = P("energy", "dom", None, None, None)
    return jax.shard_map(body, mesh=mesh, in_specs=in_specs, out_specs=out_specs, check_vma=False)
```

```python
import jax
import jax.numpy as jnp
from jax import lax
from jax.sharding import PartitionSpec as P

BW = 32


emission_weight = 1.3
absorb_weight = 0.3
couple_scale = 0.04
broaden = 0.02
lead_gamma = 0.1
lead_scale = 0.1

HI = lax.Precision.HIGHEST


def symmetric(matrix):
    return 0.5 * (matrix + jnp.swapaxes(matrix, -1, -2))


def invert_pair(block_re, block_im):
    orbitals = block_re.shape[-1]
    eye_mat = jnp.eye(orbitals, dtype=block_re.dtype)
    first_factor = jnp.linalg.cholesky(block_re)
    solved = lax.linalg.triangular_solve(
        first_factor, jnp.concatenate([block_im, eye_mat], axis=1), left_side=True, lower=True
    )
    ratio_half, first_inverse = solved[:, :orbitals], solved[:, orbitals:]
    merged = symmetric(block_re + jnp.dot(ratio_half.T, ratio_half, precision=HI))
    second_factor = jnp.linalg.cholesky(merged)
    second_inverse = lax.linalg.triangular_solve(second_factor, eye_mat, left_side=True, lower=True)
    inv_re = jnp.dot(second_inverse.T, second_inverse, precision=HI)
    inv_im = jnp.dot(first_inverse.T, jnp.dot(ratio_half, inv_re, precision=HI), precision=HI)
    return (inv_re, inv_im)


def slab_blocks(hamiltonian, coupling, deform, fetched, energy, first_mask, last_mask):
    orbitals = hamiltonian.shape[-1]
    positions = jnp.arange(orbitals)
    distance = jnp.abs(positions[:, None] - positions[None, :]).astype(hamiltonian.dtype)
    profile = jnp.where(distance <= BW, jnp.exp(-2.0 * distance / BW), 0.0)
    weight = couple_scale * deform[:, :, None] * deform[:, None, :] * profile
    mixed_part = symmetric(fetched)
    sigma_re = weight * mixed_part[:, 0]
    sigma_im = weight * mixed_part[:, 1]
    eye_mat = jnp.eye(orbitals, dtype=hamiltonian.dtype)
    lead_term = lead_scale * jnp.matmul(jnp.swapaxes(coupling, 1, 2), coupling, precision=HI)
    block_re = hamiltonian - energy * eye_mat + sigma_re
    block_im = (
        broaden * eye_mat
        - sigma_im
        + first_mask[:, None, None] * lead_gamma * eye_mat
        + last_mask[:, None, None] * lead_term
    )
    return (block_re, block_im)


def partner_levels(energy_level, phonon_offsets, level_count):
    lower_level = energy_level - phonon_offsets[0, energy_level]
    upper_level = energy_level + phonon_offsets[1, energy_level]
    lower_level = jnp.where(lower_level >= 0, lower_level, -1)
    upper_level = jnp.where(upper_level < level_count, upper_level, -1)
    return (lower_level, upper_level)


def body(hamiltonian, coupling, deform, green_prev, energy_grid, slot_energy, phonon_offsets):
    local_slabs = hamiltonian.shape[0]
    level_count = slot_energy.shape[0]
    dom_count = lax.axis_size("dom")
    dom_index = lax.axis_index("dom")
    slab_total = local_slabs * dom_count
    own_slot = lax.axis_index("energy")
    energy_level = slot_energy[own_slot]
    energy = energy_grid[energy_level]
    lower_level, upper_level = partner_levels(energy_level, phonon_offsets, level_count)
    weights = emission_weight * (slot_energy == lower_level).astype(jnp.float32) + absorb_weight * (
        slot_energy == upper_level
    ).astype(jnp.float32)
    fetched = jnp.einsum(
        "n,nsabc->sabc",
        weights,
        lax.all_gather(green_prev, "energy", axis=0, tiled=True).astype(jnp.float32),
        precision=HI,
    )
    global_index = dom_index * local_slabs + jnp.arange(local_slabs)
    first_mask = (global_index == 0).astype(jnp.float32)
    last_mask = (global_index == slab_total - 1).astype(jnp.float32)
    block_re, block_im = slab_blocks(
        hamiltonian, coupling, deform, fetched, energy, first_mask, last_mask
    )
    gathered = lax.all_gather(
        jnp.stack([block_re, block_im, coupling]), "dom", axis=1, tiled=True
    )
    all_re, all_im, all_link = gathered[0], gathered[1], gathered[2]
    orbitals = hamiltonian.shape[-1]
    zero_block = jnp.zeros((orbitals, orbitals), jnp.float32)

    outputs = []
    for local in range(local_slabs):
        own = dom_index * local_slabs + local

        def chain_step(step, carry):
            left_re, left_im, right_re, right_im, out_re, out_im = carry
            is_left = step < own
            is_final = step == slab_total - 1
            slab = jnp.where(is_left, step, slab_total - 1 - step + own)
            use_left = jnp.logical_or(is_left, is_final)
            use_right = jnp.logical_not(is_left)
            in_re = all_re[slab] + jnp.where(use_left, left_re, 0.0) + jnp.where(use_right, right_re, 0.0)
            in_im = all_im[slab] + jnp.where(use_left, left_im, 0.0) + jnp.where(use_right, right_im, 0.0)
            inv_re, inv_im = invert_pair(in_re, in_im)
            link_index = jnp.where(is_left, step, jnp.maximum(slab - 1, 0))
            link_block = all_link[link_index]
            link_block = jnp.where(is_left, link_block, link_block.T)
            next_re = -symmetric(
                jnp.dot(link_block.T, jnp.dot(inv_re, link_block, precision=HI), precision=HI)
            )
            next_im = symmetric(
                jnp.dot(link_block.T, jnp.dot(inv_im, link_block, precision=HI), precision=HI)
            )
            left_re = jnp.where(is_left, next_re, left_re)
            left_im = jnp.where(is_left, next_im, left_im)
            keep_right = jnp.logical_or(is_left, is_final)
            right_re = jnp.where(keep_right, right_re, next_re)
            right_im = jnp.where(keep_right, right_im, next_im)
            return (left_re, left_im, right_re, right_im, inv_re, inv_im)

        carry = lax.fori_loop(0, slab_total, chain_step, (zero_block,) * 6)
        outputs.append(jnp.stack([-carry[4], -carry[5]]))
    return jnp.stack(outputs)[None]


def solution(mesh):
    in_specs = (
        P("dom", None, None),
        P("dom", None, None),
        P("dom", None),
        P("energy", "dom", None, None, None),
        P(),
        P(),
        P(),
    )
    out_specs = P("energy", "dom", None, None, None)
    return jax.shard_map(body, mesh=mesh, in_specs=in_specs, out_specs=out_specs, check_vma=False)
```

```python
import jax
import jax.numpy as jnp
from jax import lax
from jax.experimental import pallas as pl
from jax.experimental.pallas import tpu as pltpu
from jax.sharding import PartitionSpec as P

BW = 32


emission_weight = 1.3
absorb_weight = 0.3
couple_scale = 0.04
broaden = 0.02
lead_gamma = 0.1
lead_scale = 0.1

HI = lax.Precision.HIGHEST


def symmetric(matrix):
    return 0.5 * (matrix + jnp.swapaxes(matrix, -1, -2))


def sweep_kernel(a_ref, o_ref):
    n = a_ref.shape[0]
    half = n // 2
    o_ref[...] = a_ref[...]

    def pivot(k, carry):
        lanes = lax.broadcasted_iota(jnp.int32, (1, n), 1)
        half_cols = lax.broadcasted_iota(jnp.int32, (n, half), 1)
        a = o_ref[...]
        row = o_ref[pl.ds(k, 1), :]
        diag = jnp.sum(jnp.where(lanes == k, row, 0.0), axis=1, keepdims=True)
        inv_d = 1.0 / diag
        tile = jnp.where(k < half, a[:, :half], a[:, half:])
        col = jnp.sum(jnp.where(half_cols == lax.rem(k, half), tile, 0.0), axis=1, keepdims=True)
        scaled = row * inv_d
        factor = jnp.where(lanes == k, 1.0 - inv_d, scaled)
        o_ref[...] = a - col * factor
        o_ref[pl.ds(k, 1), :] = jnp.where(lanes == k, -inv_d, scaled)
        return carry

    lax.fori_loop(0, n, pivot, 0)


def neg_inverse(matrix):
    n = matrix.shape[-1]
    return pl.pallas_call(
        sweep_kernel,
        out_shape=jax.ShapeDtypeStruct((n, n), jnp.float32),
        in_specs=[pl.BlockSpec(memory_space=pltpu.VMEM)],
        out_specs=pl.BlockSpec(memory_space=pltpu.VMEM),
    )(matrix)


def invert_pair(block_re, block_im):
    first_neg = neg_inverse(block_re)
    solved_ratio = -jnp.dot(first_neg, block_im, precision=HI)
    merged = symmetric(block_re + jnp.dot(block_im, solved_ratio, precision=HI))
    inv_re = -neg_inverse(merged)
    inv_im = jnp.dot(solved_ratio, inv_re, precision=HI)
    return (inv_re, inv_im)


def slab_blocks(hamiltonian, coupling, deform, fetched, energy, first_mask, last_mask):
    orbitals = hamiltonian.shape[-1]
    positions = jnp.arange(orbitals)
    distance = jnp.abs(positions[:, None] - positions[None, :]).astype(hamiltonian.dtype)
    profile = jnp.where(distance <= BW, jnp.exp(-2.0 * distance / BW), 0.0)
    weight = couple_scale * deform[:, :, None] * deform[:, None, :] * profile
    mixed_part = symmetric(fetched)
    sigma_re = weight * mixed_part[:, 0]
    sigma_im = weight * mixed_part[:, 1]
    eye_mat = jnp.eye(orbitals, dtype=hamiltonian.dtype)
    lead_term = lead_scale * jnp.matmul(jnp.swapaxes(coupling, 1, 2), coupling, precision=HI)
    block_re = hamiltonian - energy * eye_mat + sigma_re
    block_im = (
        broaden * eye_mat
        - sigma_im
        + first_mask[:, None, None] * lead_gamma * eye_mat
        + last_mask[:, None, None] * lead_term
    )
    return (block_re, block_im)


def partner_levels(energy_level, phonon_offsets, level_count):
    lower_level = energy_level - phonon_offsets[0, energy_level]
    upper_level = energy_level + phonon_offsets[1, energy_level]
    lower_level = jnp.where(lower_level >= 0, lower_level, -1)
    upper_level = jnp.where(upper_level < level_count, upper_level, -1)
    return (lower_level, upper_level)


def body(hamiltonian, coupling, deform, green_prev, energy_grid, slot_energy, phonon_offsets):
    local_slabs = hamiltonian.shape[0]
    level_count = slot_energy.shape[0]
    dom_count = lax.axis_size("dom")
    dom_index = lax.axis_index("dom")
    slab_total = local_slabs * dom_count
    own_slot = lax.axis_index("energy")
    energy_level = slot_energy[own_slot]
    energy = energy_grid[energy_level]
    lower_level, upper_level = partner_levels(energy_level, phonon_offsets, level_count)
    weights = emission_weight * (slot_energy == lower_level).astype(jnp.float32) + absorb_weight * (
        slot_energy == upper_level
    ).astype(jnp.float32)
    fetched = jnp.einsum(
        "n,nsabc->sabc",
        weights,
        lax.all_gather(green_prev, "energy", axis=0, tiled=True).astype(jnp.float32),
        precision=HI,
    )
    global_index = dom_index * local_slabs + jnp.arange(local_slabs)
    first_mask = (global_index == 0).astype(jnp.float32)
    last_mask = (global_index == slab_total - 1).astype(jnp.float32)
    block_re, block_im = slab_blocks(
        hamiltonian, coupling, deform, fetched, energy, first_mask, last_mask
    )
    gathered = lax.all_gather(
        jnp.stack([block_re, block_im, coupling]), "dom", axis=1, tiled=True
    )
    all_re, all_im, all_link = gathered[0], gathered[1], gathered[2]
    orbitals = hamiltonian.shape[-1]
    zero_block = jnp.zeros((orbitals, orbitals), jnp.float32)

    outputs = []
    for local in range(local_slabs):
        own = dom_index * local_slabs + local

        def chain_step(step, carry):
            left_re, left_im, right_re, right_im, out_re, out_im = carry
            is_left = step < own
            is_final = step == slab_total - 1
            slab = jnp.where(is_left, step, slab_total - 1 - step + own)
            use_left = jnp.logical_or(is_left, is_final)
            use_right = jnp.logical_not(is_left)
            in_re = all_re[slab] + jnp.where(use_left, left_re, 0.0) + jnp.where(use_right, right_re, 0.0)
            in_im = all_im[slab] + jnp.where(use_left, left_im, 0.0) + jnp.where(use_right, right_im, 0.0)
            inv_re, inv_im = invert_pair(in_re, in_im)
            link_index = jnp.where(is_left, step, jnp.maximum(slab - 1, 0))
            link_block = all_link[link_index]
            link_block = jnp.where(is_left, link_block, link_block.T)
            next_re = -symmetric(
                jnp.dot(link_block.T, jnp.dot(inv_re, link_block, precision=HI), precision=HI)
            )
            next_im = symmetric(
                jnp.dot(link_block.T, jnp.dot(inv_im, link_block, precision=HI), precision=HI)
            )
            left_re = jnp.where(is_left, next_re, left_re)
            left_im = jnp.where(is_left, next_im, left_im)
            keep_right = jnp.logical_or(is_left, is_final)
            right_re = jnp.where(keep_right, right_re, next_re)
            right_im = jnp.where(keep_right, right_im, next_im)
            return (left_re, left_im, right_re, right_im, inv_re, inv_im)

        carry = lax.fori_loop(0, slab_total, chain_step, (zero_block,) * 6)
        outputs.append(jnp.stack([-carry[4], -carry[5]]))
    return jnp.stack(outputs)[None]


def solution(mesh):
    in_specs = (
        P("dom", None, None),
        P("dom", None, None),
        P("dom", None),
        P("energy", "dom", None, None, None),
        P(),
        P(),
        P(),
    )
    out_specs = P("energy", "dom", None, None, None)
    return jax.shard_map(body, mesh=mesh, in_specs=in_specs, out_specs=out_specs, check_vma=False)
```

```python
import jax
import jax.numpy as jnp
from jax import lax
from jax.experimental import pallas as pl
from jax.experimental.pallas import tpu as pltpu
from jax.sharding import PartitionSpec as P

BW = 32


emission_weight = 1.3
absorb_weight = 0.3
couple_scale = 0.04
broaden = 0.02
lead_gamma = 0.1
lead_scale = 0.1

HI = lax.Precision.HIGHEST


def symmetric(matrix):
    return 0.5 * (matrix + jnp.swapaxes(matrix, -1, -2))


def sweep_kernel(ar_ref, ai_ref, or_ref, oi_ref):
    n = ar_ref.shape[0]
    half = n // 2
    or_ref[...] = ar_ref[...]
    oi_ref[...] = ai_ref[...]

    def pivot(k, carry):
        lanes = lax.broadcasted_iota(jnp.int32, (1, n), 1)
        half_cols = lax.broadcasted_iota(jnp.int32, (n, half), 1)
        kh = lax.rem(k, half)
        at_k = lanes == k
        a_re = or_ref[...]
        a_im = oi_ref[...]
        row_re = or_ref[pl.ds(k, 1), :]
        row_im = oi_ref[pl.ds(k, 1), :]
        d_re = jnp.sum(jnp.where(at_k, row_re, 0.0), axis=1, keepdims=True)
        d_im = jnp.sum(jnp.where(at_k, row_im, 0.0), axis=1, keepdims=True)
        tile_re = jnp.where(k < half, a_re[:, :half], a_re[:, half:])
        tile_im = jnp.where(k < half, a_im[:, :half], a_im[:, half:])
        col_re = jnp.sum(jnp.where(half_cols == kh, tile_re, 0.0), axis=1, keepdims=True)
        col_im = jnp.sum(jnp.where(half_cols == kh, tile_im, 0.0), axis=1, keepdims=True)
        norm = d_re * d_re + d_im * d_im
        inv_re = d_re / norm
        inv_im = -d_im / norm
        s_re = row_re * inv_re - row_im * inv_im
        s_im = row_re * inv_im + row_im * inv_re
        f_re = jnp.where(at_k, 1.0 - inv_re, s_re)
        f_im = jnp.where(at_k, -inv_im, s_im)
        or_ref[...] = a_re - (col_re * f_re - col_im * f_im)
        oi_ref[...] = a_im - (col_re * f_im + col_im * f_re)
        or_ref[pl.ds(k, 1), :] = jnp.where(at_k, -inv_re, s_re)
        oi_ref[pl.ds(k, 1), :] = jnp.where(at_k, -inv_im, s_im)
        return carry

    lax.fori_loop(0, n, pivot, 0)


def invert_pair(block_re, block_im):
    n = block_re.shape[-1]
    spec = pl.BlockSpec(memory_space=pltpu.VMEM)
    neg_re, neg_im = pl.pallas_call(
        sweep_kernel,
        out_shape=(jax.ShapeDtypeStruct((n, n), jnp.float32),) * 2,
        in_specs=[spec, spec],
        out_specs=(spec, spec),
    )(block_re, -block_im)
    return (-neg_re, -neg_im)


def slab_blocks(hamiltonian, coupling, deform, fetched, energy, first_mask, last_mask):
    orbitals = hamiltonian.shape[-1]
    positions = jnp.arange(orbitals)
    distance = jnp.abs(positions[:, None] - positions[None, :]).astype(hamiltonian.dtype)
    profile = jnp.where(distance <= BW, jnp.exp(-2.0 * distance / BW), 0.0)
    weight = couple_scale * deform[:, :, None] * deform[:, None, :] * profile
    mixed_part = symmetric(fetched)
    sigma_re = weight * mixed_part[:, 0]
    sigma_im = weight * mixed_part[:, 1]
    eye_mat = jnp.eye(orbitals, dtype=hamiltonian.dtype)
    lead_term = lead_scale * jnp.matmul(jnp.swapaxes(coupling, 1, 2), coupling, precision=HI)
    block_re = hamiltonian - energy * eye_mat + sigma_re
    block_im = (
        broaden * eye_mat
        - sigma_im
        + first_mask[:, None, None] * lead_gamma * eye_mat
        + last_mask[:, None, None] * lead_term
    )
    return (block_re, block_im)


def partner_levels(energy_level, phonon_offsets, level_count):
    lower_level = energy_level - phonon_offsets[0, energy_level]
    upper_level = energy_level + phonon_offsets[1, energy_level]
    lower_level = jnp.where(lower_level >= 0, lower_level, -1)
    upper_level = jnp.where(upper_level < level_count, upper_level, -1)
    return (lower_level, upper_level)


def body(hamiltonian, coupling, deform, green_prev, energy_grid, slot_energy, phonon_offsets):
    local_slabs = hamiltonian.shape[0]
    level_count = slot_energy.shape[0]
    dom_count = lax.axis_size("dom")
    dom_index = lax.axis_index("dom")
    slab_total = local_slabs * dom_count
    own_slot = lax.axis_index("energy")
    energy_level = slot_energy[own_slot]
    energy = energy_grid[energy_level]
    lower_level, upper_level = partner_levels(energy_level, phonon_offsets, level_count)
    weights = emission_weight * (slot_energy == lower_level).astype(jnp.float32) + absorb_weight * (
        slot_energy == upper_level
    ).astype(jnp.float32)
    fetched = jnp.einsum(
        "n,nsabc->sabc",
        weights,
        lax.all_gather(green_prev, "energy", axis=0, tiled=True).astype(jnp.float32),
        precision=HI,
    )
    global_index = dom_index * local_slabs + jnp.arange(local_slabs)
    first_mask = (global_index == 0).astype(jnp.float32)
    last_mask = (global_index == slab_total - 1).astype(jnp.float32)
    block_re, block_im = slab_blocks(
        hamiltonian, coupling, deform, fetched, energy, first_mask, last_mask
    )
    gathered = lax.all_gather(
        jnp.stack([block_re, block_im, coupling]), "dom", axis=1, tiled=True
    )
    all_re, all_im, all_link = gathered[0], gathered[1], gathered[2]
    orbitals = hamiltonian.shape[-1]
    zero_block = jnp.zeros((orbitals, orbitals), jnp.float32)

    outputs = []
    for local in range(local_slabs):
        own = dom_index * local_slabs + local

        def chain_step(step, carry):
            left_re, left_im, right_re, right_im, out_re, out_im = carry
            is_left = step < own
            is_final = step == slab_total - 1
            slab = jnp.where(is_left, step, slab_total - 1 - step + own)
            use_left = jnp.logical_or(is_left, is_final)
            use_right = jnp.logical_not(is_left)
            in_re = all_re[slab] + jnp.where(use_left, left_re, 0.0) + jnp.where(use_right, right_re, 0.0)
            in_im = all_im[slab] + jnp.where(use_left, left_im, 0.0) + jnp.where(use_right, right_im, 0.0)
            inv_re, inv_im = invert_pair(in_re, in_im)
            link_index = jnp.where(is_left, step, jnp.maximum(slab - 1, 0))
            link_block = all_link[link_index]
            link_block = jnp.where(is_left, link_block, link_block.T)
            next_re = -symmetric(
                jnp.dot(link_block.T, jnp.dot(inv_re, link_block, precision=HI), precision=HI)
            )
            next_im = symmetric(
                jnp.dot(link_block.T, jnp.dot(inv_im, link_block, precision=HI), precision=HI)
            )
            left_re = jnp.where(is_left, next_re, left_re)
            left_im = jnp.where(is_left, next_im, left_im)
            keep_right = jnp.logical_or(is_left, is_final)
            right_re = jnp.where(keep_right, right_re, next_re)
            right_im = jnp.where(keep_right, right_im, next_im)
            return (left_re, left_im, right_re, right_im, inv_re, inv_im)

        carry = lax.fori_loop(0, slab_total, chain_step, (zero_block,) * 6)
        outputs.append(jnp.stack([-carry[4], -carry[5]]))
    return jnp.stack(outputs)[None]


def solution(mesh):
    in_specs = (
        P("dom", None, None),
        P("dom", None, None),
        P("dom", None),
        P("energy", "dom", None, None, None),
        P(),
        P(),
        P(),
    )
    out_specs = P("energy", "dom", None, None, None)
    return jax.shard_map(body, mesh=mesh, in_specs=in_specs, out_specs=out_specs, check_vma=False)
```

```python
import jax
import jax.numpy as jnp
from jax import lax
from jax.experimental import pallas as pl
from jax.experimental.pallas import tpu as pltpu
from jax.sharding import PartitionSpec as P

BW = 32


emission_weight = 1.3
absorb_weight = 0.3
couple_scale = 0.04
broaden = 0.02
lead_gamma = 0.1
lead_scale = 0.1

HI = lax.Precision.HIGHEST


def symmetric(matrix):
    return 0.5 * (matrix + jnp.swapaxes(matrix, -1, -2))


def sweep_kernel(ar_ref, ai_ref, or_ref, oi_ref):
    n = ar_ref.shape[0]
    half = n // 2
    or_ref[...] = ar_ref[...]
    oi_ref[...] = ai_ref[...]

    def pivot(k, carry):
        lanes = lax.broadcasted_iota(jnp.int32, (1, n), 1)
        half_cols = lax.broadcasted_iota(jnp.int32, (n, half), 1)
        kh = lax.rem(k, half)
        at_k = lanes == k
        a_re = or_ref[...]
        a_im = oi_ref[...]
        row_re = or_ref[pl.ds(k, 1), :]
        row_im = oi_ref[pl.ds(k, 1), :]
        d_re = jnp.sum(jnp.where(at_k, row_re, 0.0), axis=1, keepdims=True)
        d_im = jnp.sum(jnp.where(at_k, row_im, 0.0), axis=1, keepdims=True)
        tile_re = jnp.where(k < half, a_re[:, :half], a_re[:, half:])
        tile_im = jnp.where(k < half, a_im[:, :half], a_im[:, half:])
        col_re = jnp.sum(jnp.where(half_cols == kh, tile_re, 0.0), axis=1, keepdims=True)
        col_im = jnp.sum(jnp.where(half_cols == kh, tile_im, 0.0), axis=1, keepdims=True)
        norm = d_re * d_re + d_im * d_im
        inv_re = d_re / norm
        inv_im = -d_im / norm
        s_re = row_re * inv_re - row_im * inv_im
        s_im = row_re * inv_im + row_im * inv_re
        f_re = jnp.where(at_k, 1.0 - inv_re, s_re)
        f_im = jnp.where(at_k, -inv_im, s_im)
        or_ref[...] = a_re - (col_re * f_re - col_im * f_im)
        oi_ref[...] = a_im - (col_re * f_im + col_im * f_re)
        or_ref[pl.ds(k, 1), :] = jnp.where(at_k, -inv_re, s_re)
        oi_ref[pl.ds(k, 1), :] = jnp.where(at_k, -inv_im, s_im)
        return carry

    lax.fori_loop(0, n, pivot, 0)


def invert_pair(block_re, block_im):
    n = block_re.shape[-1]
    spec = pl.BlockSpec(memory_space=pltpu.VMEM)
    neg_re, neg_im = pl.pallas_call(
        sweep_kernel,
        out_shape=(jax.ShapeDtypeStruct((n, n), jnp.float32),) * 2,
        in_specs=[spec, spec],
        out_specs=(spec, spec),
    )(block_re, -block_im)
    return (-neg_re, -neg_im)


def slab_blocks(hamiltonian, deform, fetched, energy, first_mask, last_mask, lead_term):
    orbitals = hamiltonian.shape[-1]
    positions = jnp.arange(orbitals)
    distance = jnp.abs(positions[:, None] - positions[None, :]).astype(hamiltonian.dtype)
    profile = jnp.where(distance <= BW, jnp.exp(-2.0 * distance / BW), 0.0)
    weight = couple_scale * deform[:, :, None] * deform[:, None, :] * profile
    mixed_part = symmetric(fetched)
    sigma_re = weight * mixed_part[:, 0]
    sigma_im = weight * mixed_part[:, 1]
    eye_mat = jnp.eye(orbitals, dtype=hamiltonian.dtype)
    block_re = hamiltonian - energy * eye_mat + sigma_re
    block_im = (
        broaden * eye_mat
        - sigma_im
        + first_mask[:, None, None] * lead_gamma * eye_mat
        + last_mask[:, None, None] * lead_term[None]
    )
    return (block_re, block_im)


def partner_levels(energy_level, phonon_offsets, level_count):
    lower_level = energy_level - phonon_offsets[0, energy_level]
    upper_level = energy_level + phonon_offsets[1, energy_level]
    lower_level = jnp.where(lower_level >= 0, lower_level, -1)
    upper_level = jnp.where(upper_level < level_count, upper_level, -1)
    return (lower_level, upper_level)


def band_windows(orbitals):
    rows = BW
    width = rows + 2 * BW
    if orbitals % rows or width > orbitals:
        return None
    return [(r * rows, min(max(r * rows - BW, 0), orbitals - width)) for r in range(orbitals // rows)], rows, width


def pack_band(matrix, windows):
    spots, rows, width = windows
    return jnp.stack([matrix[..., r0:r0 + rows, c0:c0 + width] for r0, c0 in spots], axis=-3)


def unpack_band(packed, windows, orbitals):
    spots, rows, width = windows
    pieces = []
    for index, (r0, c0) in enumerate(spots):
        pad = [(0, 0)] * (packed.ndim - 3) + [(0, 0), (c0, orbitals - c0 - width)]
        pieces.append(jnp.pad(packed[..., index, :, :], pad))
    return jnp.concatenate(pieces, axis=-2)


def body(hamiltonian, coupling, deform, green_prev, energy_grid, slot_energy, phonon_offsets):
    local_slabs = hamiltonian.shape[0]
    orbitals = hamiltonian.shape[-1]
    level_count = slot_energy.shape[0]
    dom_count = lax.axis_size("dom")
    dom_index = lax.axis_index("dom")
    slab_total = local_slabs * dom_count
    dense = lax.all_gather(jnp.stack([hamiltonian, coupling]), "dom", axis=1, tiled=True)
    all_deform = lax.all_gather(deform, "dom", axis=0, tiled=True)
    windows = band_windows(orbitals)
    shipped = green_prev if windows is None else pack_band(green_prev, windows)
    gathered = lax.all_gather(shipped, "energy", axis=0, tiled=True)
    own_slot = lax.axis_index("energy")
    energy_level = slot_energy[own_slot]
    energy = energy_grid[energy_level]
    lower_level, upper_level = partner_levels(energy_level, phonon_offsets, level_count)
    lower_slot = jnp.argmax(slot_energy == jnp.maximum(lower_level, 0))
    upper_slot = jnp.argmax(slot_energy == jnp.maximum(upper_level, 0))
    low_weight = jnp.where(lower_level >= 0, emission_weight, 0.0)
    high_weight = jnp.where(upper_level >= 0, absorb_weight, 0.0)
    fetched = low_weight * gathered[lower_slot].astype(jnp.float32) + high_weight * gathered[
        upper_slot
    ].astype(jnp.float32)
    all_fetched = lax.all_gather(fetched, "dom", axis=0, tiled=True)
    if windows is not None:
        all_fetched = unpack_band(all_fetched, windows, orbitals)
    all_link = dense[1]
    last_link = all_link[slab_total - 1]
    lead_term = lead_scale * jnp.matmul(last_link.T, last_link, precision=HI)
    global_index = jnp.arange(slab_total)
    first_mask = (global_index == 0).astype(jnp.float32)
    last_mask = (global_index == slab_total - 1).astype(jnp.float32)
    all_re, all_im = slab_blocks(
        dense[0], all_deform, all_fetched, energy, first_mask, last_mask, lead_term
    )
    zero_block = jnp.zeros((orbitals, orbitals), jnp.float32)

    outputs = []
    for local in range(local_slabs):
        own = dom_index * local_slabs + local

        def chain_step(step, carry):
            left_re, left_im, right_re, right_im, out_re, out_im = carry
            is_left = step < own
            is_final = step == slab_total - 1
            slab = jnp.where(is_left, step, slab_total - 1 - step + own)
            use_left = jnp.logical_or(is_left, is_final)
            use_right = jnp.logical_not(is_left)
            in_re = all_re[slab] + jnp.where(use_left, left_re, 0.0) + jnp.where(use_right, right_re, 0.0)
            in_im = all_im[slab] + jnp.where(use_left, left_im, 0.0) + jnp.where(use_right, right_im, 0.0)
            inv_re, inv_im = invert_pair(in_re, in_im)
            link_index = jnp.where(is_left, step, jnp.maximum(slab - 1, 0))
            link_block = all_link[link_index]
            link_block = jnp.where(is_left, link_block, link_block.T)
            next_re = -symmetric(
                jnp.dot(link_block.T, jnp.dot(inv_re, link_block, precision=HI), precision=HI)
            )
            next_im = symmetric(
                jnp.dot(link_block.T, jnp.dot(inv_im, link_block, precision=HI), precision=HI)
            )
            left_re = jnp.where(is_left, next_re, left_re)
            left_im = jnp.where(is_left, next_im, left_im)
            keep_right = jnp.logical_or(is_left, is_final)
            right_re = jnp.where(keep_right, right_re, next_re)
            right_im = jnp.where(keep_right, right_im, next_im)
            return (left_re, left_im, right_re, right_im, inv_re, inv_im)

        carry = lax.fori_loop(0, slab_total, chain_step, (zero_block,) * 6)
        outputs.append(jnp.stack([-carry[4], -carry[5]]))
    return jnp.stack(outputs)[None]


def solution(mesh):
    in_specs = (
        P("dom", None, None),
        P("dom", None, None),
        P("dom", None),
        P("energy", "dom", None, None, None),
        P(),
        P(),
        P(),
    )
    out_specs = P("energy", "dom", None, None, None)
    return jax.shard_map(body, mesh=mesh, in_specs=in_specs, out_specs=out_specs, check_vma=False)
```

```python
import jax
import jax.numpy as jnp
from jax import lax
from jax.experimental import pallas as pl
from jax.experimental.pallas import tpu as pltpu
from jax.sharding import PartitionSpec as P

BW = 32


emission_weight = 1.3
absorb_weight = 0.3
couple_scale = 0.04
broaden = 0.02
lead_gamma = 0.1
lead_scale = 0.1

HI = lax.Precision.HIGHEST


def symmetric(matrix):
    return 0.5 * (matrix + jnp.swapaxes(matrix, -1, -2))


def sweep_kernel(ar_ref, ai_ref, or_ref, oi_ref):
    n = ar_ref.shape[0]
    half = n // 2
    or_ref[...] = ar_ref[...]
    oi_ref[...] = ai_ref[...]

    def pivot(k, carry):
        lanes = lax.broadcasted_iota(jnp.int32, (1, n), 1)
        half_cols = lax.broadcasted_iota(jnp.int32, (n, half), 1)
        kh = lax.rem(k, half)
        at_k = lanes == k
        a_re = or_ref[...]
        a_im = oi_ref[...]
        row_re = or_ref[pl.ds(k, 1), :]
        row_im = oi_ref[pl.ds(k, 1), :]
        d_re = jnp.sum(jnp.where(at_k, row_re, 0.0), axis=1, keepdims=True)
        d_im = jnp.sum(jnp.where(at_k, row_im, 0.0), axis=1, keepdims=True)
        tile_re = jnp.where(k < half, a_re[:, :half], a_re[:, half:])
        tile_im = jnp.where(k < half, a_im[:, :half], a_im[:, half:])
        col_re = jnp.sum(jnp.where(half_cols == kh, tile_re, 0.0), axis=1, keepdims=True)
        col_im = jnp.sum(jnp.where(half_cols == kh, tile_im, 0.0), axis=1, keepdims=True)
        norm = d_re * d_re + d_im * d_im
        inv_re = d_re / norm
        inv_im = -d_im / norm
        s_re = row_re * inv_re - row_im * inv_im
        s_im = row_re * inv_im + row_im * inv_re
        f_re = jnp.where(at_k, 1.0 - inv_re, s_re)
        f_im = jnp.where(at_k, -inv_im, s_im)
        or_ref[...] = a_re - (col_re * f_re - col_im * f_im)
        oi_ref[...] = a_im - (col_re * f_im + col_im * f_re)
        or_ref[pl.ds(k, 1), :] = jnp.where(at_k, -inv_re, s_re)
        oi_ref[pl.ds(k, 1), :] = jnp.where(at_k, -inv_im, s_im)
        return carry

    lax.fori_loop(0, n, pivot, 0)


def invert_pair(block_re, block_im):
    n = block_re.shape[-1]
    spec = pl.BlockSpec(memory_space=pltpu.VMEM)
    neg_re, neg_im = pl.pallas_call(
        sweep_kernel,
        out_shape=(jax.ShapeDtypeStruct((n, n), jnp.float32),) * 2,
        in_specs=[spec, spec],
        out_specs=(spec, spec),
    )(block_re, -block_im)
    return (-neg_re, -neg_im)


def slab_blocks(hamiltonian, coupling, deform, fetched, energy, first_mask, last_mask):
    orbitals = hamiltonian.shape[-1]
    positions = jnp.arange(orbitals)
    distance = jnp.abs(positions[:, None] - positions[None, :]).astype(hamiltonian.dtype)
    profile = jnp.where(distance <= BW, jnp.exp(-2.0 * distance / BW), 0.0)
    weight = couple_scale * deform[:, :, None] * deform[:, None, :] * profile
    mixed_part = symmetric(fetched)
    sigma_re = weight * mixed_part[:, 0]
    sigma_im = weight * mixed_part[:, 1]
    eye_mat = jnp.eye(orbitals, dtype=hamiltonian.dtype)
    lead_term = lead_scale * jnp.matmul(jnp.swapaxes(coupling, 1, 2), coupling, precision=HI)
    block_re = hamiltonian - energy * eye_mat + sigma_re
    block_im = (
        broaden * eye_mat
        - sigma_im
        + first_mask[:, None, None] * lead_gamma * eye_mat
        + last_mask[:, None, None] * lead_term
    )
    return (block_re, block_im)


def gathered_over_dom(array):
    peers = lax.axis_size("dom")
    pieces = [array]
    for shift in range(1, peers):
        pairs = [(i, (i + shift) % peers) for i in range(peers)]
        pieces.append(lax.ppermute(array, "dom", pairs))
    order = (lax.axis_index("dom") - jnp.arange(peers)) % peers
    stacked = jnp.stack(pieces)[order]
    return stacked.reshape((peers * array.shape[0],) + array.shape[1:])


def partner_levels(energy_level, phonon_offsets, level_count):
    lower_level = energy_level - phonon_offsets[0, energy_level]
    upper_level = energy_level + phonon_offsets[1, energy_level]
    lower_level = jnp.where(lower_level >= 0, lower_level, -1)
    upper_level = jnp.where(upper_level < level_count, upper_level, -1)
    return (lower_level, upper_level)


def body(hamiltonian, coupling, deform, green_prev, energy_grid, slot_energy, phonon_offsets):
    local_slabs = hamiltonian.shape[0]
    orbitals = hamiltonian.shape[-1]
    level_count = slot_energy.shape[0]
    dom_count = lax.axis_size("dom")
    dom_index = lax.axis_index("dom")
    slab_total = local_slabs * dom_count
    all_link = gathered_over_dom(coupling)
    gathered = lax.all_gather(green_prev, "energy", axis=0, tiled=True)
    own_slot = lax.axis_index("energy")
    energy_level = slot_energy[own_slot]
    energy = energy_grid[energy_level]
    lower_level, upper_level = partner_levels(energy_level, phonon_offsets, level_count)
    lower_slot = jnp.argmax(slot_energy == jnp.maximum(lower_level, 0))
    upper_slot = jnp.argmax(slot_energy == jnp.maximum(upper_level, 0))
    low_weight = jnp.where(lower_level >= 0, emission_weight, 0.0)
    high_weight = jnp.where(upper_level >= 0, absorb_weight, 0.0)
    fetched = low_weight * gathered[lower_slot].astype(jnp.float32) + high_weight * gathered[
        upper_slot
    ].astype(jnp.float32)
    global_index = dom_index * local_slabs + jnp.arange(local_slabs)
    first_mask = (global_index == 0).astype(jnp.float32)
    last_mask = (global_index == slab_total - 1).astype(jnp.float32)
    block_re, block_im = slab_blocks(
        hamiltonian, coupling, deform, fetched, energy, first_mask, last_mask
    )
    blocks = lax.all_gather(jnp.stack([block_re, block_im]), "dom", axis=1, tiled=True)
    all_re, all_im = blocks[0], blocks[1]
    zero_block = jnp.zeros((orbitals, orbitals), jnp.float32)

    outputs = []
    for local in range(local_slabs):
        own = dom_index * local_slabs + local

        def chain_step(step, carry):
            left_re, left_im, right_re, right_im, out_re, out_im = carry
            is_left = step < own
            is_final = step == slab_total - 1
            slab = jnp.where(is_left, step, slab_total - 1 - step + own)
            use_left = jnp.logical_or(is_left, is_final)
            use_right = jnp.logical_not(is_left)
            in_re = all_re[slab] + jnp.where(use_left, left_re, 0.0) + jnp.where(use_right, right_re, 0.0)
            in_im = all_im[slab] + jnp.where(use_left, left_im, 0.0) + jnp.where(use_right, right_im, 0.0)
            inv_re, inv_im = invert_pair(in_re, in_im)
            link_index = jnp.where(is_left, step, jnp.maximum(slab - 1, 0))
            link_block = all_link[link_index]
            link_block = jnp.where(is_left, link_block, link_block.T)
            next_re = -symmetric(
                jnp.dot(link_block.T, jnp.dot(inv_re, link_block, precision=HI), precision=HI)
            )
            next_im = symmetric(
                jnp.dot(link_block.T, jnp.dot(inv_im, link_block, precision=HI), precision=HI)
            )
            left_re = jnp.where(is_left, next_re, left_re)
            left_im = jnp.where(is_left, next_im, left_im)
            keep_right = jnp.logical_or(is_left, is_final)
            right_re = jnp.where(keep_right, right_re, next_re)
            right_im = jnp.where(keep_right, right_im, next_im)
            return (left_re, left_im, right_re, right_im, inv_re, inv_im)

        carry = lax.fori_loop(0, slab_total, chain_step, (zero_block,) * 6)
        outputs.append(jnp.stack([-carry[4], -carry[5]]))
    return jnp.stack(outputs)[None]


def solution(mesh):
    in_specs = (
        P("dom", None, None),
        P("dom", None, None),
        P("dom", None),
        P("energy", "dom", None, None, None),
        P(),
        P(),
        P(),
    )
    out_specs = P("energy", "dom", None, None, None)
    return jax.shard_map(body, mesh=mesh, in_specs=in_specs, out_specs=out_specs, check_vma=False)
```

```python
import jax
import jax.numpy as jnp
from jax import lax
from jax.experimental import pallas as pl
from jax.experimental.pallas import tpu as pltpu
from jax.sharding import PartitionSpec as P

BW = 32


emission_weight = 1.3
absorb_weight = 0.3
couple_scale = 0.04
broaden = 0.02
lead_gamma = 0.1
lead_scale = 0.1

HI = lax.Precision.HIGHEST


def symmetric(matrix):
    return 0.5 * (matrix + jnp.swapaxes(matrix, -1, -2))


def sweep_kernel(
    scalars, blk_re_ref, blk_im_ref, lre_ref, lim_ref, rre_ref, rim_ref, or_ref, oi_ref
):
    n = or_ref.shape[0]
    half = n // 2
    use_left = scalars[1] == 1
    use_right = scalars[2] == 1
    or_ref[...] = (
        blk_re_ref[...]
        + jnp.where(use_left, lre_ref[...], 0.0)
        + jnp.where(use_right, rre_ref[...], 0.0)
    )
    oi_ref[...] = -(
        blk_im_ref[...]
        + jnp.where(use_left, lim_ref[...], 0.0)
        + jnp.where(use_right, rim_ref[...], 0.0)
    )

    def pivot(k, carry):
        lanes = lax.broadcasted_iota(jnp.int32, (1, n), 1)
        half_cols = lax.broadcasted_iota(jnp.int32, (n, half), 1)
        kh = lax.rem(k, half)
        at_k = lanes == k
        a_re = or_ref[...]
        a_im = oi_ref[...]
        row_re = or_ref[pl.ds(k, 1), :]
        row_im = oi_ref[pl.ds(k, 1), :]
        d_re = jnp.sum(jnp.where(at_k, row_re, 0.0), axis=1, keepdims=True)
        d_im = jnp.sum(jnp.where(at_k, row_im, 0.0), axis=1, keepdims=True)
        tile_re = jnp.where(k < half, a_re[:, :half], a_re[:, half:])
        tile_im = jnp.where(k < half, a_im[:, :half], a_im[:, half:])
        col_re = jnp.sum(jnp.where(half_cols == kh, tile_re, 0.0), axis=1, keepdims=True)
        col_im = jnp.sum(jnp.where(half_cols == kh, tile_im, 0.0), axis=1, keepdims=True)
        norm = d_re * d_re + d_im * d_im
        inv_re = d_re / norm
        inv_im = -d_im / norm
        s_re = row_re * inv_re - row_im * inv_im
        s_im = row_re * inv_im + row_im * inv_re
        f_re = jnp.where(at_k, 1.0 - inv_re, s_re)
        f_im = jnp.where(at_k, -inv_im, s_im)
        or_ref[...] = a_re - (col_re * f_re - col_im * f_im)
        oi_ref[...] = a_im - (col_re * f_im + col_im * f_re)
        or_ref[pl.ds(k, 1), :] = jnp.where(at_k, -inv_re, s_re)
        oi_ref[pl.ds(k, 1), :] = jnp.where(at_k, -inv_im, s_im)
        return carry

    lax.fori_loop(0, n, pivot, 0)


def neg_inverse_step(scalars, all_re, all_im, left_re, left_im, right_re, right_im):
    n = all_re.shape[-1]
    slab_spec = pl.BlockSpec((None, n, n), lambda i, sc: (sc[0], 0, 0))
    full_spec = pl.BlockSpec((n, n), lambda i, sc: (0, 0))
    grid_spec = pltpu.PrefetchScalarGridSpec(
        num_scalar_prefetch=1,
        grid=(1,),
        in_specs=[slab_spec, slab_spec, full_spec, full_spec, full_spec, full_spec],
        out_specs=[full_spec, full_spec],
    )
    return pl.pallas_call(
        sweep_kernel,
        out_shape=(jax.ShapeDtypeStruct((n, n), jnp.float32),) * 2,
        grid_spec=grid_spec,
    )(scalars, all_re, all_im, left_re, left_im, right_re, right_im)


def slab_blocks(hamiltonian, coupling, deform, fetched, energy, first_mask, last_mask):
    orbitals = hamiltonian.shape[-1]
    positions = jnp.arange(orbitals)
    distance = jnp.abs(positions[:, None] - positions[None, :]).astype(hamiltonian.dtype)
    profile = jnp.where(distance <= BW, jnp.exp(-2.0 * distance / BW), 0.0)
    weight = couple_scale * deform[:, :, None] * deform[:, None, :] * profile
    mixed_part = symmetric(fetched)
    sigma_re = weight * mixed_part[:, 0]
    sigma_im = weight * mixed_part[:, 1]
    eye_mat = jnp.eye(orbitals, dtype=hamiltonian.dtype)
    lead_term = lead_scale * jnp.matmul(jnp.swapaxes(coupling, 1, 2), coupling, precision=HI)
    block_re = hamiltonian - energy * eye_mat + sigma_re
    block_im = (
        broaden * eye_mat
        - sigma_im
        + first_mask[:, None, None] * lead_gamma * eye_mat
        + last_mask[:, None, None] * lead_term
    )
    return (block_re, block_im)


def gathered_over_dom(array):
    peers = lax.axis_size("dom")
    pieces = [array]
    for shift in range(1, peers):
        pairs = [(i, (i + shift) % peers) for i in range(peers)]
        pieces.append(lax.ppermute(array, "dom", pairs))
    order = (lax.axis_index("dom") - jnp.arange(peers)) % peers
    stacked = jnp.stack(pieces)[order]
    return stacked.reshape((peers * array.shape[0],) + array.shape[1:])


def partner_levels(energy_level, phonon_offsets, level_count):
    lower_level = energy_level - phonon_offsets[0, energy_level]
    upper_level = energy_level + phonon_offsets[1, energy_level]
    lower_level = jnp.where(lower_level >= 0, lower_level, -1)
    upper_level = jnp.where(upper_level < level_count, upper_level, -1)
    return (lower_level, upper_level)


def body(hamiltonian, coupling, deform, green_prev, energy_grid, slot_energy, phonon_offsets):
    local_slabs = hamiltonian.shape[0]
    orbitals = hamiltonian.shape[-1]
    level_count = slot_energy.shape[0]
    dom_count = lax.axis_size("dom")
    dom_index = lax.axis_index("dom")
    slab_total = local_slabs * dom_count
    all_link = gathered_over_dom(coupling)
    gathered = lax.all_gather(green_prev, "energy", axis=0, tiled=True)
    own_slot = lax.axis_index("energy")
    energy_level = slot_energy[own_slot]
    energy = energy_grid[energy_level]
    lower_level, upper_level = partner_levels(energy_level, phonon_offsets, level_count)
    lower_slot = jnp.argmax(slot_energy == jnp.maximum(lower_level, 0))
    upper_slot = jnp.argmax(slot_energy == jnp.maximum(upper_level, 0))
    low_weight = jnp.where(lower_level >= 0, emission_weight, 0.0)
    high_weight = jnp.where(upper_level >= 0, absorb_weight, 0.0)
    fetched = low_weight * gathered[lower_slot].astype(jnp.float32) + high_weight * gathered[
        upper_slot
    ].astype(jnp.float32)
    global_index = dom_index * local_slabs + jnp.arange(local_slabs)
    first_mask = (global_index == 0).astype(jnp.float32)
    last_mask = (global_index == slab_total - 1).astype(jnp.float32)
    block_re, block_im = slab_blocks(
        hamiltonian, coupling, deform, fetched, energy, first_mask, last_mask
    )
    blocks = lax.all_gather(jnp.stack([block_re, block_im]), "dom", axis=1, tiled=True)
    all_re, all_im = blocks[0], blocks[1]
    zero_block = jnp.zeros((orbitals, orbitals), jnp.float32)

    outputs = []
    for local in range(local_slabs):
        own = dom_index * local_slabs + local

        def chain_step(step, carry):
            left_re, left_im, right_re, right_im, out_re, out_im = carry
            is_left = step < own
            is_final = step == slab_total - 1
            slab = jnp.where(is_left, step, slab_total - 1 - step + own)
            use_left = jnp.logical_or(is_left, is_final)
            use_right = jnp.logical_not(is_left)
            scalars = jnp.stack([slab, use_left, use_right]).astype(jnp.int32)
            neg_re, neg_im = neg_inverse_step(
                scalars, all_re, all_im, left_re, left_im, right_re, right_im
            )
            link_index = jnp.where(is_left, step, jnp.maximum(slab - 1, 0))
            link_block = all_link[link_index]
            link_block = jnp.where(is_left, link_block, link_block.T)
            next_re = symmetric(
                jnp.dot(link_block.T, jnp.dot(neg_re, link_block, precision=HI), precision=HI)
            )
            next_im = -symmetric(
                jnp.dot(link_block.T, jnp.dot(neg_im, link_block, precision=HI), precision=HI)
            )
            left_re = jnp.where(is_left, next_re, left_re)
            left_im = jnp.where(is_left, next_im, left_im)
            keep_right = jnp.logical_or(is_left, is_final)
            right_re = jnp.where(keep_right, right_re, next_re)
            right_im = jnp.where(keep_right, right_im, next_im)
            return (left_re, left_im, right_re, right_im, neg_re, neg_im)

        carry = lax.fori_loop(0, slab_total, chain_step, (zero_block,) * 6)
        outputs.append(jnp.stack([carry[4], carry[5]]))
    return jnp.stack(outputs)[None]


def solution(mesh):
    in_specs = (
        P("dom", None, None),
        P("dom", None, None),
        P("dom", None),
        P("energy", "dom", None, None, None),
        P(),
        P(),
        P(),
    )
    out_specs = P("energy", "dom", None, None, None)
    return jax.shard_map(body, mesh=mesh, in_specs=in_specs, out_specs=out_specs, check_vma=False)
```

```python
import jax
import jax.numpy as jnp
from jax import lax
from jax.experimental import pallas as pl
from jax.experimental.pallas import tpu as pltpu
from jax.sharding import PartitionSpec as P

BW = 32


emission_weight = 1.3
absorb_weight = 0.3
couple_scale = 0.04
broaden = 0.02
lead_gamma = 0.1
lead_scale = 0.1

HI = lax.Precision.HIGHEST


def symmetric(matrix):
    return 0.5 * (matrix + jnp.swapaxes(matrix, -1, -2))


def sweep_kernel(ar_ref, ai_ref, or_ref, oi_ref):
    n = ar_ref.shape[0]
    half = n // 2
    or_ref[...] = ar_ref[...]
    oi_ref[...] = ai_ref[...]

    def pivot(k, carry):
        lanes = lax.broadcasted_iota(jnp.int32, (1, n), 1)
        half_cols = lax.broadcasted_iota(jnp.int32, (n, half), 1)
        kh = lax.rem(k, half)
        at_k = lanes == k
        a_re = or_ref[...]
        a_im = oi_ref[...]
        row_re = or_ref[pl.ds(k, 1), :]
        row_im = oi_ref[pl.ds(k, 1), :]
        d_re = jnp.sum(jnp.where(at_k, row_re, 0.0), axis=1, keepdims=True)
        d_im = jnp.sum(jnp.where(at_k, row_im, 0.0), axis=1, keepdims=True)
        tile_re = jnp.where(k < half, a_re[:, :half], a_re[:, half:])
        tile_im = jnp.where(k < half, a_im[:, :half], a_im[:, half:])
        col_re = jnp.sum(jnp.where(half_cols == kh, tile_re, 0.0), axis=1, keepdims=True)
        col_im = jnp.sum(jnp.where(half_cols == kh, tile_im, 0.0), axis=1, keepdims=True)
        norm = d_re * d_re + d_im * d_im
        inv_re = d_re / norm
        inv_im = -d_im / norm
        s_re = row_re * inv_re - row_im * inv_im
        s_im = row_re * inv_im + row_im * inv_re
        f_re = jnp.where(at_k, 1.0 - inv_re, s_re)
        f_im = jnp.where(at_k, -inv_im, s_im)
        or_ref[...] = a_re - (col_re * f_re - col_im * f_im)
        oi_ref[...] = a_im - (col_re * f_im + col_im * f_re)
        or_ref[pl.ds(k, 1), :] = jnp.where(at_k, -inv_re, s_re)
        oi_ref[pl.ds(k, 1), :] = jnp.where(at_k, -inv_im, s_im)
        return carry

    lax.fori_loop(0, n, pivot, 0)


def neg_invert_pair(block_re, block_im):
    n = block_re.shape[-1]
    spec = pl.BlockSpec(memory_space=pltpu.VMEM)
    neg_re, neg_im = pl.pallas_call(
        sweep_kernel,
        out_shape=(jax.ShapeDtypeStruct((n, n), jnp.float32),) * 2,
        in_specs=[spec, spec],
        out_specs=(spec, spec),
    )(block_re, -block_im)
    return (neg_re, neg_im)


def slab_blocks(hamiltonian, coupling, deform, fetched, energy, first_mask, last_mask):
    orbitals = hamiltonian.shape[-1]
    positions = jnp.arange(orbitals)
    distance = jnp.abs(positions[:, None] - positions[None, :]).astype(hamiltonian.dtype)
    profile = jnp.where(distance <= BW, jnp.exp(-2.0 * distance / BW), 0.0)
    weight = couple_scale * deform[:, :, None] * deform[:, None, :] * profile
    mixed_part = symmetric(fetched)
    sigma_re = weight * mixed_part[:, 0]
    sigma_im = weight * mixed_part[:, 1]
    eye_mat = jnp.eye(orbitals, dtype=hamiltonian.dtype)
    lead_term = lead_scale * jnp.matmul(jnp.swapaxes(coupling, 1, 2), coupling, precision=HI)
    block_re = hamiltonian - energy * eye_mat + sigma_re
    block_im = (
        broaden * eye_mat
        - sigma_im
        + first_mask[:, None, None] * lead_gamma * eye_mat
        + last_mask[:, None, None] * lead_term
    )
    return (block_re, block_im)


def gathered_over_dom(array):
    peers = lax.axis_size("dom")
    pieces = [array]
    for shift in range(1, peers):
        pairs = [(i, (i + shift) % peers) for i in range(peers)]
        pieces.append(lax.ppermute(array, "dom", pairs))
    order = (lax.axis_index("dom") - jnp.arange(peers)) % peers
    stacked = jnp.stack(pieces)[order]
    return stacked.reshape((peers * array.shape[0],) + array.shape[1:])


def partner_levels(energy_level, phonon_offsets, level_count):
    lower_level = energy_level - phonon_offsets[0, energy_level]
    upper_level = energy_level + phonon_offsets[1, energy_level]
    lower_level = jnp.where(lower_level >= 0, lower_level, -1)
    upper_level = jnp.where(upper_level < level_count, upper_level, -1)
    return (lower_level, upper_level)


def body(hamiltonian, coupling, deform, green_prev, energy_grid, slot_energy, phonon_offsets):
    local_slabs = hamiltonian.shape[0]
    orbitals = hamiltonian.shape[-1]
    level_count = slot_energy.shape[0]
    dom_count = lax.axis_size("dom")
    dom_index = lax.axis_index("dom")
    slab_total = local_slabs * dom_count
    all_link = gathered_over_dom(coupling)
    gathered = lax.all_gather(green_prev, "energy", axis=0, tiled=True)
    own_slot = lax.axis_index("energy")
    energy_level = slot_energy[own_slot]
    energy = energy_grid[energy_level]
    lower_level, upper_level = partner_levels(energy_level, phonon_offsets, level_count)
    lower_slot = jnp.argmax(slot_energy == jnp.maximum(lower_level, 0))
    upper_slot = jnp.argmax(slot_energy == jnp.maximum(upper_level, 0))
    low_weight = jnp.where(lower_level >= 0, emission_weight, 0.0)
    high_weight = jnp.where(upper_level >= 0, absorb_weight, 0.0)
    fetched = low_weight * gathered[lower_slot].astype(jnp.float32) + high_weight * gathered[
        upper_slot
    ].astype(jnp.float32)
    global_index = dom_index * local_slabs + jnp.arange(local_slabs)
    first_mask = (global_index == 0).astype(jnp.float32)
    last_mask = (global_index == slab_total - 1).astype(jnp.float32)
    block_re, block_im = slab_blocks(
        hamiltonian, coupling, deform, fetched, energy, first_mask, last_mask
    )
    blocks = lax.all_gather(jnp.stack([block_re, block_im]), "dom", axis=1, tiled=True)
    zero_block = jnp.zeros((orbitals, orbitals), jnp.float32)

    outputs = []
    for local in range(local_slabs):
        own = dom_index * local_slabs + local

        def chain_step(step, carry):
            left_re, left_im, right_re, right_im, out_re, out_im = carry
            is_left = step < own
            is_final = step == slab_total - 1
            slab = jnp.where(is_left, step, slab_total - 1 - step + own)
            use_left = jnp.logical_or(is_left, is_final)
            use_right = jnp.logical_not(is_left)
            in_re = blocks[0, slab] + jnp.where(use_left, left_re, 0.0) + jnp.where(use_right, right_re, 0.0)
            in_im = blocks[1, slab] + jnp.where(use_left, left_im, 0.0) + jnp.where(use_right, right_im, 0.0)
            neg_re, neg_im = neg_invert_pair(in_re, in_im)
            link_index = jnp.where(is_left, step, jnp.maximum(slab - 1, 0))
            link_block = all_link[link_index]
            link_block = jnp.where(is_left, link_block, link_block.T)
            next_re = symmetric(
                jnp.dot(link_block.T, jnp.dot(neg_re, link_block, precision=HI), precision=HI)
            )
            next_im = -symmetric(
                jnp.dot(link_block.T, jnp.dot(neg_im, link_block, precision=HI), precision=HI)
            )
            left_re = jnp.where(is_left, next_re, left_re)
            left_im = jnp.where(is_left, next_im, left_im)
            keep_right = jnp.logical_or(is_left, is_final)
            right_re = jnp.where(keep_right, right_re, next_re)
            right_im = jnp.where(keep_right, right_im, next_im)
            return (left_re, left_im, right_re, right_im, neg_re, neg_im)

        carry = lax.fori_loop(0, slab_total, chain_step, (zero_block,) * 6)
        outputs.append(jnp.stack([carry[4], carry[5]]))
    return jnp.stack(outputs)[None]


def solution(mesh):
    in_specs = (
        P("dom", None, None),
        P("dom", None, None),
        P("dom", None),
        P("energy", "dom", None, None, None),
        P(),
        P(),
        P(),
    )
    out_specs = P("energy", "dom", None, None, None)
    return jax.shard_map(body, mesh=mesh, in_specs=in_specs, out_specs=out_specs, check_vma=False)
```

```python
import jax
import jax.numpy as jnp
from jax import lax
from jax.experimental import pallas as pl
from jax.experimental.pallas import tpu as pltpu
from jax.sharding import PartitionSpec as P

BW = 32


emission_weight = 1.3
absorb_weight = 0.3
couple_scale = 0.04
broaden = 0.02
lead_gamma = 0.1
lead_scale = 0.1

HI = lax.Precision.HIGHEST


def symmetric(matrix):
    return 0.5 * (matrix + jnp.swapaxes(matrix, -1, -2))


def sweep_kernel(ar_ref, ai_ref, or_ref, oi_ref):
    n = ar_ref.shape[0]
    half = n // 2
    or_ref[...] = ar_ref[...]
    oi_ref[...] = ai_ref[...]

    def pivot(k, carry):
        lanes = lax.broadcasted_iota(jnp.int32, (1, n), 1)
        half_cols = lax.broadcasted_iota(jnp.int32, (n, half), 1)
        kh = lax.rem(k, half)
        at_k = lanes == k
        a_re = or_ref[...]
        a_im = oi_ref[...]
        row_re = or_ref[pl.ds(k, 1), :]
        row_im = oi_ref[pl.ds(k, 1), :]
        d_re = jnp.sum(jnp.where(at_k, row_re, 0.0), axis=1, keepdims=True)
        d_im = jnp.sum(jnp.where(at_k, row_im, 0.0), axis=1, keepdims=True)
        tile_re = jnp.where(k < half, a_re[:, :half], a_re[:, half:])
        tile_im = jnp.where(k < half, a_im[:, :half], a_im[:, half:])
        col_re = jnp.sum(jnp.where(half_cols == kh, tile_re, 0.0), axis=1, keepdims=True)
        col_im = jnp.sum(jnp.where(half_cols == kh, tile_im, 0.0), axis=1, keepdims=True)
        norm = d_re * d_re + d_im * d_im
        inv_re = d_re / norm
        inv_im = -d_im / norm
        s_re = row_re * inv_re - row_im * inv_im
        s_im = row_re * inv_im + row_im * inv_re
        f_re = jnp.where(at_k, 1.0 - inv_re, s_re)
        f_im = jnp.where(at_k, -inv_im, s_im)
        or_ref[...] = a_re - (col_re * f_re - col_im * f_im)
        oi_ref[...] = a_im - (col_re * f_im + col_im * f_re)
        or_ref[pl.ds(k, 1), :] = jnp.where(at_k, -inv_re, s_re)
        oi_ref[pl.ds(k, 1), :] = jnp.where(at_k, -inv_im, s_im)
        return carry

    lax.fori_loop(0, n, pivot, 0)


def neg_invert_pair(block_re, block_im):
    n = block_re.shape[-1]
    spec = pl.BlockSpec(memory_space=pltpu.VMEM)
    neg_re, neg_im = pl.pallas_call(
        sweep_kernel,
        out_shape=(jax.ShapeDtypeStruct((n, n), jnp.float32),) * 2,
        in_specs=[spec, spec],
        out_specs=(spec, spec),
    )(block_re, -block_im)
    return (neg_re, neg_im)


def slab_blocks(hamiltonian, coupling, deform, fetched, energy, first_mask, last_mask):
    orbitals = hamiltonian.shape[-1]
    positions = jnp.arange(orbitals)
    distance = jnp.abs(positions[:, None] - positions[None, :]).astype(hamiltonian.dtype)
    profile = jnp.where(distance <= BW, jnp.exp(-2.0 * distance / BW), 0.0)
    weight = couple_scale * deform[:, :, None] * deform[:, None, :] * profile
    mixed_part = symmetric(fetched)
    sigma_re = weight * mixed_part[:, 0]
    sigma_im = weight * mixed_part[:, 1]
    eye_mat = jnp.eye(orbitals, dtype=hamiltonian.dtype)
    lead_term = lead_scale * jnp.matmul(jnp.swapaxes(coupling, 1, 2), coupling, precision=HI)
    block_re = hamiltonian - energy * eye_mat + sigma_re
    block_im = (
        broaden * eye_mat
        - sigma_im
        + first_mask[:, None, None] * lead_gamma * eye_mat
        + last_mask[:, None, None] * lead_term
    )
    return (block_re, block_im)


def partner_levels(energy_level, phonon_offsets, level_count):
    lower_level = energy_level - phonon_offsets[0, energy_level]
    upper_level = energy_level + phonon_offsets[1, energy_level]
    lower_level = jnp.where(lower_level >= 0, lower_level, -1)
    upper_level = jnp.where(upper_level < level_count, upper_level, -1)
    return (lower_level, upper_level)


def body(hamiltonian, coupling, deform, green_prev, energy_grid, slot_energy, phonon_offsets):
    local_slabs = hamiltonian.shape[0]
    orbitals = hamiltonian.shape[-1]
    level_count = slot_energy.shape[0]
    dom_count = lax.axis_size("dom")
    dom_index = lax.axis_index("dom")
    slab_total = local_slabs * dom_count
    all_link = lax.all_gather(coupling, "dom", axis=0, tiled=True)
    all_link, green_prev = lax.optimization_barrier((all_link, green_prev))
    gathered = lax.all_gather(green_prev, "energy", axis=0, tiled=True)
    own_slot = lax.axis_index("energy")
    energy_level = slot_energy[own_slot]
    energy = energy_grid[energy_level]
    lower_level, upper_level = partner_levels(energy_level, phonon_offsets, level_count)
    lower_slot = jnp.argmax(slot_energy == jnp.maximum(lower_level, 0))
    upper_slot = jnp.argmax(slot_energy == jnp.maximum(upper_level, 0))
    low_weight = jnp.where(lower_level >= 0, emission_weight, 0.0)
    high_weight = jnp.where(upper_level >= 0, absorb_weight, 0.0)
    fetched = low_weight * gathered[lower_slot].astype(jnp.float32) + high_weight * gathered[
        upper_slot
    ].astype(jnp.float32)
    global_index = dom_index * local_slabs + jnp.arange(local_slabs)
    first_mask = (global_index == 0).astype(jnp.float32)
    last_mask = (global_index == slab_total - 1).astype(jnp.float32)
    block_re, block_im = slab_blocks(
        hamiltonian, coupling, deform, fetched, energy, first_mask, last_mask
    )
    blocks = lax.all_gather(jnp.stack([block_re, block_im]), "dom", axis=1, tiled=True)
    zero_block = jnp.zeros((orbitals, orbitals), jnp.float32)

    outputs = []
    for local in range(local_slabs):
        own = dom_index * local_slabs + local

        def chain_step(step, carry):
            left_re, left_im, right_re, right_im, out_re, out_im = carry
            is_left = step < own
            is_final = step == slab_total - 1
            slab = jnp.where(is_left, step, slab_total - 1 - step + own)
            use_left = jnp.logical_or(is_left, is_final)
            use_right = jnp.logical_not(is_left)
            in_re = blocks[0, slab] + jnp.where(use_left, left_re, 0.0) + jnp.where(use_right, right_re, 0.0)
            in_im = blocks[1, slab] + jnp.where(use_left, left_im, 0.0) + jnp.where(use_right, right_im, 0.0)
            neg_re, neg_im = neg_invert_pair(in_re, in_im)
            link_index = jnp.where(is_left, step, jnp.maximum(slab - 1, 0))
            link_block = all_link[link_index]
            link_block = jnp.where(is_left, link_block, link_block.T)
            next_re = symmetric(
                jnp.dot(link_block.T, jnp.dot(neg_re, link_block, precision=HI), precision=HI)
            )
            next_im = -symmetric(
                jnp.dot(link_block.T, jnp.dot(neg_im, link_block, precision=HI), precision=HI)
            )
            left_re = jnp.where(is_left, next_re, left_re)
            left_im = jnp.where(is_left, next_im, left_im)
            keep_right = jnp.logical_or(is_left, is_final)
            right_re = jnp.where(keep_right, right_re, next_re)
            right_im = jnp.where(keep_right, right_im, next_im)
            return (left_re, left_im, right_re, right_im, neg_re, neg_im)

        carry = lax.fori_loop(0, slab_total, chain_step, (zero_block,) * 6)
        outputs.append(jnp.stack([carry[4], carry[5]]))
    return jnp.stack(outputs)[None]


def solution(mesh):
    in_specs = (
        P("dom", None, None),
        P("dom", None, None),
        P("dom", None),
        P("energy", "dom", None, None, None),
        P(),
        P(),
        P(),
    )
    out_specs = P("energy", "dom", None, None, None)
    return jax.shard_map(body, mesh=mesh, in_specs=in_specs, out_specs=out_specs, check_vma=False)
```

```python
import jax
import jax.numpy as jnp
from jax import lax
from jax.experimental import pallas as pl
from jax.experimental.pallas import tpu as pltpu
from jax.sharding import PartitionSpec as P

BW = 32


emission_weight = 1.3
absorb_weight = 0.3
couple_scale = 0.04
broaden = 0.02
lead_gamma = 0.1
lead_scale = 0.1

HI = lax.Precision.HIGHEST


def symmetric(matrix):
    return 0.5 * (matrix + jnp.swapaxes(matrix, -1, -2))


def sweep_kernel(ar_ref, ai_ref, or_ref, oi_ref):
    n = ar_ref.shape[0]
    half = n // 2
    or_ref[...] = ar_ref[...]
    oi_ref[...] = ai_ref[...]

    def pivot(k, carry):
        lanes = lax.broadcasted_iota(jnp.int32, (1, n), 1)
        half_cols = lax.broadcasted_iota(jnp.int32, (n, half), 1)
        kh = lax.rem(k, half)
        at_k = lanes == k
        a_re = or_ref[...]
        a_im = oi_ref[...]
        row_re = or_ref[pl.ds(k, 1), :]
        row_im = oi_ref[pl.ds(k, 1), :]
        d_re = jnp.sum(jnp.where(at_k, row_re, 0.0), axis=1, keepdims=True)
        d_im = jnp.sum(jnp.where(at_k, row_im, 0.0), axis=1, keepdims=True)
        tile_re = jnp.where(k < half, a_re[:, :half], a_re[:, half:])
        tile_im = jnp.where(k < half, a_im[:, :half], a_im[:, half:])
        col_re = jnp.sum(jnp.where(half_cols == kh, tile_re, 0.0), axis=1, keepdims=True)
        col_im = jnp.sum(jnp.where(half_cols == kh, tile_im, 0.0), axis=1, keepdims=True)
        norm = d_re * d_re + d_im * d_im
        inv_re = d_re / norm
        inv_im = -d_im / norm
        s_re = row_re * inv_re - row_im * inv_im
        s_im = row_re * inv_im + row_im * inv_re
        f_re = jnp.where(at_k, 1.0 - inv_re, s_re)
        f_im = jnp.where(at_k, -inv_im, s_im)
        or_ref[...] = a_re - (col_re * f_re - col_im * f_im)
        oi_ref[...] = a_im - (col_re * f_im + col_im * f_re)
        or_ref[pl.ds(k, 1), :] = jnp.where(at_k, -inv_re, s_re)
        oi_ref[pl.ds(k, 1), :] = jnp.where(at_k, -inv_im, s_im)
        return carry

    lax.fori_loop(0, n, pivot, 0)


def neg_invert_pair(block_re, block_im):
    n = block_re.shape[-1]
    spec = pl.BlockSpec(memory_space=pltpu.VMEM)
    neg_re, neg_im = pl.pallas_call(
        sweep_kernel,
        out_shape=(jax.ShapeDtypeStruct((n, n), jnp.float32),) * 2,
        in_specs=[spec, spec],
        out_specs=(spec, spec),
    )(block_re, -block_im)
    return (neg_re, neg_im)


def slab_blocks(hamiltonian, coupling, deform, fetched, energy, first_mask, last_mask):
    orbitals = hamiltonian.shape[-1]
    positions = jnp.arange(orbitals)
    distance = jnp.abs(positions[:, None] - positions[None, :]).astype(hamiltonian.dtype)
    profile = jnp.where(distance <= BW, jnp.exp(-2.0 * distance / BW), 0.0)
    weight = couple_scale * deform[:, :, None] * deform[:, None, :] * profile
    mixed_part = symmetric(fetched)
    sigma_re = weight * mixed_part[:, 0]
    sigma_im = weight * mixed_part[:, 1]
    eye_mat = jnp.eye(orbitals, dtype=hamiltonian.dtype)
    lead_term = lead_scale * jnp.matmul(jnp.swapaxes(coupling, 1, 2), coupling, precision=HI)
    block_re = hamiltonian - energy * eye_mat + sigma_re
    block_im = (
        broaden * eye_mat
        - sigma_im
        + first_mask[:, None, None] * lead_gamma * eye_mat
        + last_mask[:, None, None] * lead_term
    )
    return (block_re, block_im)


def gathered_over_dom(array):
    peers = lax.axis_size("dom")
    pieces = [array]
    for shift in range(1, peers):
        pairs = [(i, (i + shift) % peers) for i in range(peers)]
        pieces.append(lax.ppermute(array, "dom", pairs))
    order = (lax.axis_index("dom") - jnp.arange(peers)) % peers
    stacked = jnp.stack(pieces)[order]
    return stacked.reshape((peers * array.shape[0],) + array.shape[1:])


def partner_levels(energy_level, phonon_offsets, level_count):
    lower_level = energy_level - phonon_offsets[0, energy_level]
    upper_level = energy_level + phonon_offsets[1, energy_level]
    lower_level = jnp.where(lower_level >= 0, lower_level, -1)
    upper_level = jnp.where(upper_level < level_count, upper_level, -1)
    return (lower_level, upper_level)


def body(hamiltonian, coupling, deform, green_prev, energy_grid, slot_energy, phonon_offsets):
    local_slabs = hamiltonian.shape[0]
    orbitals = hamiltonian.shape[-1]
    level_count = slot_energy.shape[0]
    dom_count = lax.axis_size("dom")
    dom_index = lax.axis_index("dom")
    slab_total = local_slabs * dom_count
    gathered = lax.all_gather(green_prev, "energy", axis=0, tiled=True)
    own_slot = lax.axis_index("energy")
    energy_level = slot_energy[own_slot]
    energy = energy_grid[energy_level]
    lower_level, upper_level = partner_levels(energy_level, phonon_offsets, level_count)
    lower_slot = jnp.argmax(slot_energy == jnp.maximum(lower_level, 0))
    upper_slot = jnp.argmax(slot_energy == jnp.maximum(upper_level, 0))
    low_weight = jnp.where(lower_level >= 0, emission_weight, 0.0)
    high_weight = jnp.where(upper_level >= 0, absorb_weight, 0.0)
    fetched = low_weight * gathered[lower_slot].astype(jnp.float32) + high_weight * gathered[
        upper_slot
    ].astype(jnp.float32)
    global_index = dom_index * local_slabs + jnp.arange(local_slabs)
    first_mask = (global_index == 0).astype(jnp.float32)
    last_mask = (global_index == slab_total - 1).astype(jnp.float32)
    block_re, block_im = slab_blocks(
        hamiltonian, coupling, deform, fetched, energy, first_mask, last_mask
    )
    blocks = gathered_over_dom(jnp.stack([block_re, block_im, coupling], axis=1))
    all_link = blocks[:, 2]
    zero_block = jnp.zeros((orbitals, orbitals), jnp.float32)

    outputs = []
    for local in range(local_slabs):
        own = dom_index * local_slabs + local

        def chain_step(step, carry):
            left_re, left_im, right_re, right_im, out_re, out_im = carry
            is_left = step < own
            is_final = step == slab_total - 1
            slab = jnp.where(is_left, step, slab_total - 1 - step + own)
            use_left = jnp.logical_or(is_left, is_final)
            use_right = jnp.logical_not(is_left)
            in_re = blocks[slab, 0] + jnp.where(use_left, left_re, 0.0) + jnp.where(use_right, right_re, 0.0)
            in_im = blocks[slab, 1] + jnp.where(use_left, left_im, 0.0) + jnp.where(use_right, right_im, 0.0)
            neg_re, neg_im = neg_invert_pair(in_re, in_im)
            link_index = jnp.where(is_left, step, jnp.maximum(slab - 1, 0))
            link_block = all_link[link_index]
            link_block = jnp.where(is_left, link_block, link_block.T)
            next_re = symmetric(
                jnp.dot(link_block.T, jnp.dot(neg_re, link_block, precision=HI), precision=HI)
            )
            next_im = -symmetric(
                jnp.dot(link_block.T, jnp.dot(neg_im, link_block, precision=HI), precision=HI)
            )
            left_re = jnp.where(is_left, next_re, left_re)
            left_im = jnp.where(is_left, next_im, left_im)
            keep_right = jnp.logical_or(is_left, is_final)
            right_re = jnp.where(keep_right, right_re, next_re)
            right_im = jnp.where(keep_right, right_im, next_im)
            return (left_re, left_im, right_re, right_im, neg_re, neg_im)

        carry = lax.fori_loop(0, slab_total, chain_step, (zero_block,) * 6)
        outputs.append(jnp.stack([carry[4], carry[5]]))
    return jnp.stack(outputs)[None]


def solution(mesh):
    in_specs = (
        P("dom", None, None),
        P("dom", None, None),
        P("dom", None),
        P("energy", "dom", None, None, None),
        P(),
        P(),
        P(),
    )
    out_specs = P("energy", "dom", None, None, None)
    return jax.shard_map(body, mesh=mesh, in_specs=in_specs, out_specs=out_specs, check_vma=False)
```

```python
import jax
import jax.numpy as jnp
from jax import lax
from jax.experimental import pallas as pl
from jax.experimental.pallas import tpu as pltpu
from jax.sharding import PartitionSpec as P

BW = 32


emission_weight = 1.3
absorb_weight = 0.3
couple_scale = 0.04
broaden = 0.02
lead_gamma = 0.1
lead_scale = 0.1

HI = lax.Precision.HIGHEST


def symmetric(matrix):
    return 0.5 * (matrix + jnp.swapaxes(matrix, -1, -2))


def sweep_kernel(ar_ref, ai_ref, or_ref, oi_ref):
    n = ar_ref.shape[0]
    half = n // 2
    or_ref[...] = ar_ref[...]
    oi_ref[...] = ai_ref[...]

    def pivot(k, carry):
        lanes = lax.broadcasted_iota(jnp.int32, (1, n), 1)
        half_cols = lax.broadcasted_iota(jnp.int32, (n, half), 1)
        kh = lax.rem(k, half)
        at_k = lanes == k
        a_re = or_ref[...]
        a_im = oi_ref[...]
        row_re = or_ref[pl.ds(k, 1), :]
        row_im = oi_ref[pl.ds(k, 1), :]
        d_re = jnp.sum(jnp.where(at_k, row_re, 0.0), axis=1, keepdims=True)
        d_im = jnp.sum(jnp.where(at_k, row_im, 0.0), axis=1, keepdims=True)
        lane_base = pl.multiple_of((k // half) * half, half)
        tile_re = or_ref[:, pl.ds(lane_base, half)]
        tile_im = oi_ref[:, pl.ds(lane_base, half)]
        col_re = jnp.sum(jnp.where(half_cols == kh, tile_re, 0.0), axis=1, keepdims=True)
        col_im = jnp.sum(jnp.where(half_cols == kh, tile_im, 0.0), axis=1, keepdims=True)
        norm = d_re * d_re + d_im * d_im
        inv_re = d_re / norm
        inv_im = -d_im / norm
        s_re = row_re * inv_re - row_im * inv_im
        s_im = row_re * inv_im + row_im * inv_re
        f_re = jnp.where(at_k, 1.0 - inv_re, s_re)
        f_im = jnp.where(at_k, -inv_im, s_im)
        or_ref[...] = a_re - (col_re * f_re - col_im * f_im)
        oi_ref[...] = a_im - (col_re * f_im + col_im * f_re)
        or_ref[pl.ds(k, 1), :] = jnp.where(at_k, -inv_re, s_re)
        oi_ref[pl.ds(k, 1), :] = jnp.where(at_k, -inv_im, s_im)
        return carry

    lax.fori_loop(0, n, pivot, 0)


def neg_invert_pair(block_re, block_im):
    n = block_re.shape[-1]
    spec = pl.BlockSpec(memory_space=pltpu.VMEM)
    neg_re, neg_im = pl.pallas_call(
        sweep_kernel,
        out_shape=(jax.ShapeDtypeStruct((n, n), jnp.float32),) * 2,
        in_specs=[spec, spec],
        out_specs=(spec, spec),
    )(block_re, -block_im)
    return (neg_re, neg_im)


def slab_blocks(hamiltonian, coupling, deform, fetched, energy, first_mask, last_mask):
    orbitals = hamiltonian.shape[-1]
    positions = jnp.arange(orbitals)
    distance = jnp.abs(positions[:, None] - positions[None, :]).astype(hamiltonian.dtype)
    profile = jnp.where(distance <= BW, jnp.exp(-2.0 * distance / BW), 0.0)
    weight = couple_scale * deform[:, :, None] * deform[:, None, :] * profile
    mixed_part = symmetric(fetched)
    sigma_re = weight * mixed_part[:, 0]
    sigma_im = weight * mixed_part[:, 1]
    eye_mat = jnp.eye(orbitals, dtype=hamiltonian.dtype)
    lead_term = lead_scale * jnp.matmul(jnp.swapaxes(coupling, 1, 2), coupling, precision=HI)
    block_re = hamiltonian - energy * eye_mat + sigma_re
    block_im = (
        broaden * eye_mat
        - sigma_im
        + first_mask[:, None, None] * lead_gamma * eye_mat
        + last_mask[:, None, None] * lead_term
    )
    return (block_re, block_im)


def gathered_over_dom(array):
    peers = lax.axis_size("dom")
    pieces = [array]
    for shift in range(1, peers):
        pairs = [(i, (i + shift) % peers) for i in range(peers)]
        pieces.append(lax.ppermute(array, "dom", pairs))
    order = (lax.axis_index("dom") - jnp.arange(peers)) % peers
    stacked = jnp.stack(pieces)[order]
    return stacked.reshape((peers * array.shape[0],) + array.shape[1:])


def partner_levels(energy_level, phonon_offsets, level_count):
    lower_level = energy_level - phonon_offsets[0, energy_level]
    upper_level = energy_level + phonon_offsets[1, energy_level]
    lower_level = jnp.where(lower_level >= 0, lower_level, -1)
    upper_level = jnp.where(upper_level < level_count, upper_level, -1)
    return (lower_level, upper_level)


def body(hamiltonian, coupling, deform, green_prev, energy_grid, slot_energy, phonon_offsets):
    local_slabs = hamiltonian.shape[0]
    orbitals = hamiltonian.shape[-1]
    level_count = slot_energy.shape[0]
    dom_count = lax.axis_size("dom")
    dom_index = lax.axis_index("dom")
    slab_total = local_slabs * dom_count
    all_link = gathered_over_dom(coupling)
    gathered = lax.all_gather(green_prev, "energy", axis=0, tiled=True)
    own_slot = lax.axis_index("energy")
    energy_level = slot_energy[own_slot]
    energy = energy_grid[energy_level]
    lower_level, upper_level = partner_levels(energy_level, phonon_offsets, level_count)
    lower_slot = jnp.argmax(slot_energy == jnp.maximum(lower_level, 0))
    upper_slot = jnp.argmax(slot_energy == jnp.maximum(upper_level, 0))
    low_weight = jnp.where(lower_level >= 0, emission_weight, 0.0)
    high_weight = jnp.where(upper_level >= 0, absorb_weight, 0.0)
    fetched = low_weight * gathered[lower_slot].astype(jnp.float32) + high_weight * gathered[
        upper_slot
    ].astype(jnp.float32)
    global_index = dom_index * local_slabs + jnp.arange(local_slabs)
    first_mask = (global_index == 0).astype(jnp.float32)
    last_mask = (global_index == slab_total - 1).astype(jnp.float32)
    block_re, block_im = slab_blocks(
        hamiltonian, coupling, deform, fetched, energy, first_mask, last_mask
    )
    blocks = lax.all_gather(jnp.stack([block_re, block_im]), "dom", axis=1, tiled=True)
    zero_block = jnp.zeros((orbitals, orbitals), jnp.float32)

    outputs = []
    for local in range(local_slabs):
        own = dom_index * local_slabs + local

        def chain_step(step, carry):
            left_re, left_im, right_re, right_im, out_re, out_im = carry
            is_left = step < own
            is_final = step == slab_total - 1
            slab = jnp.where(is_left, step, slab_total - 1 - step + own)
            use_left = jnp.logical_or(is_left, is_final)
            use_right = jnp.logical_not(is_left)
            in_re = blocks[0, slab] + jnp.where(use_left, left_re, 0.0) + jnp.where(use_right, right_re, 0.0)
            in_im = blocks[1, slab] + jnp.where(use_left, left_im, 0.0) + jnp.where(use_right, right_im, 0.0)
            neg_re, neg_im = neg_invert_pair(in_re, in_im)
            link_index = jnp.where(is_left, step, jnp.maximum(slab - 1, 0))
            link_block = all_link[link_index]
            link_block = jnp.where(is_left, link_block, link_block.T)
            next_re = symmetric(
                jnp.dot(link_block.T, jnp.dot(neg_re, link_block, precision=HI), precision=HI)
            )
            next_im = -symmetric(
                jnp.dot(link_block.T, jnp.dot(neg_im, link_block, precision=HI), precision=HI)
            )
            left_re = jnp.where(is_left, next_re, left_re)
            left_im = jnp.where(is_left, next_im, left_im)
            keep_right = jnp.logical_or(is_left, is_final)
            right_re = jnp.where(keep_right, right_re, next_re)
            right_im = jnp.where(keep_right, right_im, next_im)
            return (left_re, left_im, right_re, right_im, neg_re, neg_im)

        carry = lax.fori_loop(0, slab_total, chain_step, (zero_block,) * 6)
        outputs.append(jnp.stack([carry[4], carry[5]]))
    return jnp.stack(outputs)[None]


def solution(mesh):
    in_specs = (
        P("dom", None, None),
        P("dom", None, None),
        P("dom", None),
        P("energy", "dom", None, None, None),
        P(),
        P(),
        P(),
    )
    out_specs = P("energy", "dom", None, None, None)
    return jax.shard_map(body, mesh=mesh, in_specs=in_specs, out_specs=out_specs, check_vma=False)
```

```python
import jax
import jax.numpy as jnp
from jax import lax
from jax.experimental import pallas as pl
from jax.experimental.pallas import tpu as pltpu
from jax.sharding import PartitionSpec as P

BW = 32


emission_weight = 1.3
absorb_weight = 0.3
couple_scale = 0.04
broaden = 0.02
lead_gamma = 0.1
lead_scale = 0.1

HI = lax.Precision.HIGHEST


def symmetric(matrix):
    return 0.5 * (matrix + jnp.swapaxes(matrix, -1, -2))


def sweep_kernel(ar_ref, ai_ref, or_ref, oi_ref):
    n = ar_ref.shape[0]
    half = n // 2
    or_ref[...] = ar_ref[...]
    oi_ref[...] = ai_ref[...]

    def pivot(k, carry):
        lanes = lax.broadcasted_iota(jnp.int32, (1, n), 1)
        half_cols = lax.broadcasted_iota(jnp.int32, (n, half), 1)
        kh = lax.rem(k, half)
        at_k = lanes == k
        a_re = or_ref[...]
        a_im = oi_ref[...]
        row_re = or_ref[pl.ds(k, 1), :]
        row_im = oi_ref[pl.ds(k, 1), :]
        d_re = jnp.sum(jnp.where(at_k, row_re, 0.0), axis=1, keepdims=True)
        d_im = jnp.sum(jnp.where(at_k, row_im, 0.0), axis=1, keepdims=True)
        lane_base = pl.multiple_of((k // half) * half, half)
        tile_re = or_ref[:, pl.ds(lane_base, half)]
        tile_im = oi_ref[:, pl.ds(lane_base, half)]
        col_re = jnp.sum(jnp.where(half_cols == kh, tile_re, 0.0), axis=1, keepdims=True)
        col_im = jnp.sum(jnp.where(half_cols == kh, tile_im, 0.0), axis=1, keepdims=True)
        norm = d_re * d_re + d_im * d_im
        inv_re = d_re / norm
        inv_im = -d_im / norm
        s_re = row_re * inv_re - row_im * inv_im
        s_im = row_re * inv_im + row_im * inv_re
        f_re = jnp.where(at_k, 1.0 - inv_re, s_re)
        f_im = jnp.where(at_k, -inv_im, s_im)
        or_ref[...] = a_re - (col_re * f_re - col_im * f_im)
        oi_ref[...] = a_im - (col_re * f_im + col_im * f_re)
        or_ref[pl.ds(k, 1), :] = jnp.where(at_k, -inv_re, s_re)
        oi_ref[pl.ds(k, 1), :] = jnp.where(at_k, -inv_im, s_im)
        return carry

    lax.fori_loop(0, n, pivot, 0)


def neg_invert_pair(block_re, block_im):
    n = block_re.shape[-1]
    spec = pl.BlockSpec(memory_space=pltpu.VMEM)
    neg_re, neg_im = pl.pallas_call(
        sweep_kernel,
        out_shape=(jax.ShapeDtypeStruct((n, n), jnp.float32),) * 2,
        in_specs=[spec, spec],
        out_specs=(spec, spec),
    )(block_re, -block_im)
    return (neg_re, neg_im)


def slab_blocks(hamiltonian, coupling, deform, fetched, energy, first_mask, last_mask):
    orbitals = hamiltonian.shape[-1]
    positions = jnp.arange(orbitals)
    distance = jnp.abs(positions[:, None] - positions[None, :]).astype(hamiltonian.dtype)
    profile = jnp.where(distance <= BW, jnp.exp(-2.0 * distance / BW), 0.0)
    weight = couple_scale * deform[:, :, None] * deform[:, None, :] * profile
    mixed_part = symmetric(fetched)
    sigma_re = weight * mixed_part[:, 0]
    sigma_im = weight * mixed_part[:, 1]
    eye_mat = jnp.eye(orbitals, dtype=hamiltonian.dtype)
    lead_term = lead_scale * jnp.matmul(jnp.swapaxes(coupling, 1, 2), coupling, precision=HI)
    block_re = hamiltonian - energy * eye_mat + sigma_re
    block_im = (
        broaden * eye_mat
        - sigma_im
        + first_mask[:, None, None] * lead_gamma * eye_mat
        + last_mask[:, None, None] * lead_term
    )
    return (block_re, block_im)


def gathered_over_dom(array):
    peers = lax.axis_size("dom")
    pieces = [array]
    for shift in range(1, peers):
        pairs = [(i, (i + shift) % peers) for i in range(peers)]
        pieces.append(lax.ppermute(array, "dom", pairs))
    order = (lax.axis_index("dom") - jnp.arange(peers)) % peers
    stacked = jnp.stack(pieces)[order]
    return stacked.reshape((peers * array.shape[0],) + array.shape[1:])


def partner_levels(energy_level, phonon_offsets, level_count):
    lower_level = energy_level - phonon_offsets[0, energy_level]
    upper_level = energy_level + phonon_offsets[1, energy_level]
    lower_level = jnp.where(lower_level >= 0, lower_level, -1)
    upper_level = jnp.where(upper_level < level_count, upper_level, -1)
    return (lower_level, upper_level)


def body(hamiltonian, coupling, deform, green_prev, energy_grid, slot_energy, phonon_offsets):
    local_slabs = hamiltonian.shape[0]
    orbitals = hamiltonian.shape[-1]
    level_count = slot_energy.shape[0]
    dom_count = lax.axis_size("dom")
    dom_index = lax.axis_index("dom")
    slab_total = local_slabs * dom_count
    all_link = gathered_over_dom(coupling)
    gathered = lax.all_gather(green_prev, "energy", axis=0, tiled=True)
    own_slot = lax.axis_index("energy")
    energy_level = slot_energy[own_slot]
    energy = energy_grid[energy_level]
    lower_level, upper_level = partner_levels(energy_level, phonon_offsets, level_count)
    lower_slot = jnp.argmax(slot_energy == jnp.maximum(lower_level, 0))
    upper_slot = jnp.argmax(slot_energy == jnp.maximum(upper_level, 0))
    low_weight = jnp.where(lower_level >= 0, emission_weight, 0.0)
    high_weight = jnp.where(upper_level >= 0, absorb_weight, 0.0)
    fetched = low_weight * gathered[lower_slot].astype(jnp.float32) + high_weight * gathered[
        upper_slot
    ].astype(jnp.float32)
    global_index = dom_index * local_slabs + jnp.arange(local_slabs)
    first_mask = (global_index == 0).astype(jnp.float32)
    last_mask = (global_index == slab_total - 1).astype(jnp.float32)
    block_re, block_im = slab_blocks(
        hamiltonian, coupling, deform, fetched, energy, first_mask, last_mask
    )
    blocks = lax.all_gather(jnp.stack([block_re, block_im]), "dom", axis=1, tiled=True)
    zero_block = jnp.zeros((orbitals, orbitals), jnp.float32)

    outputs = []
    for local in range(local_slabs):
        own = dom_index * local_slabs + local

        def chain_step(step, carry):
            left_re, left_im, right_re, right_im = carry
            is_left = step < own
            slab = jnp.where(is_left, step, slab_total - 1 - step + own)
            in_re = blocks[0, slab] + jnp.where(is_left, left_re, right_re)
            in_im = blocks[1, slab] + jnp.where(is_left, left_im, right_im)
            neg_re, neg_im = neg_invert_pair(in_re, in_im)
            link_index = jnp.where(is_left, step, jnp.maximum(slab - 1, 0))
            link_block = all_link[link_index]
            link_block = jnp.where(is_left, link_block, link_block.T)
            next_re = symmetric(
                jnp.dot(link_block.T, jnp.dot(neg_re, link_block, precision=HI), precision=HI)
            )
            next_im = -symmetric(
                jnp.dot(link_block.T, jnp.dot(neg_im, link_block, precision=HI), precision=HI)
            )
            left_re = jnp.where(is_left, next_re, left_re)
            left_im = jnp.where(is_left, next_im, left_im)
            right_re = jnp.where(is_left, right_re, next_re)
            right_im = jnp.where(is_left, right_im, next_im)
            return (left_re, left_im, right_re, right_im)

        left_re, left_im, right_re, right_im = lax.fori_loop(
            0, slab_total - 1, chain_step, (zero_block,) * 4
        )
        neg_re, neg_im = neg_invert_pair(
            blocks[0, own] + left_re + right_re, blocks[1, own] + left_im + right_im
        )
        outputs.append(jnp.stack([neg_re, neg_im]))
    return jnp.stack(outputs)[None]


def solution(mesh):
    in_specs = (
        P("dom", None, None),
        P("dom", None, None),
        P("dom", None),
        P("energy", "dom", None, None, None),
        P(),
        P(),
        P(),
    )
    out_specs = P("energy", "dom", None, None, None)
    return jax.shard_map(body, mesh=mesh, in_specs=in_specs, out_specs=out_specs, check_vma=False)
```

```python
import jax
import jax.numpy as jnp
from jax import lax
from jax.experimental import pallas as pl
from jax.experimental.pallas import tpu as pltpu
from jax.sharding import PartitionSpec as P

BW = 32


emission_weight = 1.3
absorb_weight = 0.3
couple_scale = 0.04
broaden = 0.02
lead_gamma = 0.1
lead_scale = 0.1

HI = lax.Precision.HIGHEST
LINK = lax.Precision.HIGH


def symmetric(matrix):
    return 0.5 * (matrix + jnp.swapaxes(matrix, -1, -2))


def sweep_kernel(ar_ref, ai_ref, or_ref, oi_ref):
    n = ar_ref.shape[0]
    half = n // 2
    or_ref[...] = ar_ref[...]
    oi_ref[...] = ai_ref[...]

    def pivot(k, carry):
        lanes = lax.broadcasted_iota(jnp.int32, (1, n), 1)
        half_cols = lax.broadcasted_iota(jnp.int32, (n, half), 1)
        kh = lax.rem(k, half)
        at_k = lanes == k
        a_re = or_ref[...]
        a_im = oi_ref[...]
        row_re = or_ref[pl.ds(k, 1), :]
        row_im = oi_ref[pl.ds(k, 1), :]
        d_re = jnp.sum(jnp.where(at_k, row_re, 0.0), axis=1, keepdims=True)
        d_im = jnp.sum(jnp.where(at_k, row_im, 0.0), axis=1, keepdims=True)
        lane_base = pl.multiple_of((k // half) * half, half)
        tile_re = or_ref[:, pl.ds(lane_base, half)]
        tile_im = oi_ref[:, pl.ds(lane_base, half)]
        col_re = jnp.sum(jnp.where(half_cols == kh, tile_re, 0.0), axis=1, keepdims=True)
        col_im = jnp.sum(jnp.where(half_cols == kh, tile_im, 0.0), axis=1, keepdims=True)
        norm = d_re * d_re + d_im * d_im
        inv_re = d_re / norm
        inv_im = -d_im / norm
        s_re = row_re * inv_re - row_im * inv_im
        s_im = row_re * inv_im + row_im * inv_re
        f_re = jnp.where(at_k, 1.0 - inv_re, s_re)
        f_im = jnp.where(at_k, -inv_im, s_im)
        or_ref[...] = a_re - (col_re * f_re - col_im * f_im)
        oi_ref[...] = a_im - (col_re * f_im + col_im * f_re)
        or_ref[pl.ds(k, 1), :] = jnp.where(at_k, -inv_re, s_re)
        oi_ref[pl.ds(k, 1), :] = jnp.where(at_k, -inv_im, s_im)
        return carry

    lax.fori_loop(0, n, pivot, 0)


def neg_invert_pair(block_re, block_im):
    n = block_re.shape[-1]
    spec = pl.BlockSpec(memory_space=pltpu.VMEM)
    neg_re, neg_im = pl.pallas_call(
        sweep_kernel,
        out_shape=(jax.ShapeDtypeStruct((n, n), jnp.float32),) * 2,
        in_specs=[spec, spec],
        out_specs=(spec, spec),
    )(block_re, -block_im)
    return (neg_re, neg_im)


def slab_blocks(hamiltonian, coupling, deform, fetched, energy, first_mask, last_mask):
    orbitals = hamiltonian.shape[-1]
    positions = jnp.arange(orbitals)
    distance = jnp.abs(positions[:, None] - positions[None, :]).astype(hamiltonian.dtype)
    profile = jnp.where(distance <= BW, jnp.exp(-2.0 * distance / BW), 0.0)
    weight = couple_scale * deform[:, :, None] * deform[:, None, :] * profile
    mixed_part = symmetric(fetched)
    sigma_re = weight * mixed_part[:, 0]
    sigma_im = weight * mixed_part[:, 1]
    eye_mat = jnp.eye(orbitals, dtype=hamiltonian.dtype)
    lead_term = lead_scale * jnp.matmul(jnp.swapaxes(coupling, 1, 2), coupling, precision=HI)
    block_re = hamiltonian - energy * eye_mat + sigma_re
    block_im = (
        broaden * eye_mat
        - sigma_im
        + first_mask[:, None, None] * lead_gamma * eye_mat
        + last_mask[:, None, None] * lead_term
    )
    return (block_re, block_im)


def gathered_over_dom(array):
    peers = lax.axis_size("dom")
    pieces = [array]
    for shift in range(1, peers):
        pairs = [(i, (i + shift) % peers) for i in range(peers)]
        pieces.append(lax.ppermute(array, "dom", pairs))
    order = (lax.axis_index("dom") - jnp.arange(peers)) % peers
    stacked = jnp.stack(pieces)[order]
    return stacked.reshape((peers * array.shape[0],) + array.shape[1:])


def partner_levels(energy_level, phonon_offsets, level_count):
    lower_level = energy_level - phonon_offsets[0, energy_level]
    upper_level = energy_level + phonon_offsets[1, energy_level]
    lower_level = jnp.where(lower_level >= 0, lower_level, -1)
    upper_level = jnp.where(upper_level < level_count, upper_level, -1)
    return (lower_level, upper_level)


def body(hamiltonian, coupling, deform, green_prev, energy_grid, slot_energy, phonon_offsets):
    local_slabs = hamiltonian.shape[0]
    orbitals = hamiltonian.shape[-1]
    level_count = slot_energy.shape[0]
    dom_count = lax.axis_size("dom")
    dom_index = lax.axis_index("dom")
    slab_total = local_slabs * dom_count
    all_link = gathered_over_dom(coupling)
    gathered = lax.all_gather(green_prev, "energy", axis=0, tiled=True)
    own_slot = lax.axis_index("energy")
    energy_level = slot_energy[own_slot]
    energy = energy_grid[energy_level]
    lower_level, upper_level = partner_levels(energy_level, phonon_offsets, level_count)
    lower_slot = jnp.argmax(slot_energy == jnp.maximum(lower_level, 0))
    upper_slot = jnp.argmax(slot_energy == jnp.maximum(upper_level, 0))
    low_weight = jnp.where(lower_level >= 0, emission_weight, 0.0)
    high_weight = jnp.where(upper_level >= 0, absorb_weight, 0.0)
    fetched = low_weight * gathered[lower_slot].astype(jnp.float32) + high_weight * gathered[
        upper_slot
    ].astype(jnp.float32)
    global_index = dom_index * local_slabs + jnp.arange(local_slabs)
    first_mask = (global_index == 0).astype(jnp.float32)
    last_mask = (global_index == slab_total - 1).astype(jnp.float32)
    block_re, block_im = slab_blocks(
        hamiltonian, coupling, deform, fetched, energy, first_mask, last_mask
    )
    blocks = lax.all_gather(jnp.stack([block_re, block_im]), "dom", axis=1, tiled=True)
    zero_block = jnp.zeros((orbitals, orbitals), jnp.float32)

    outputs = []
    for local in range(local_slabs):
        own = dom_index * local_slabs + local

        def chain_step(step, carry):
            left_re, left_im, right_re, right_im, out_re, out_im = carry
            is_left = step < own
            is_final = step == slab_total - 1
            slab = jnp.where(is_left, step, slab_total - 1 - step + own)
            use_left = jnp.logical_or(is_left, is_final)
            use_right = jnp.logical_not(is_left)
            in_re = blocks[0, slab] + jnp.where(use_left, left_re, 0.0) + jnp.where(use_right, right_re, 0.0)
            in_im = blocks[1, slab] + jnp.where(use_left, left_im, 0.0) + jnp.where(use_right, right_im, 0.0)
            neg_re, neg_im = neg_invert_pair(in_re, in_im)
            link_index = jnp.where(is_left, step, jnp.maximum(slab - 1, 0))
            link_block = all_link[link_index]
            link_block = jnp.where(is_left, link_block, link_block.T)
            next_re = symmetric(
                jnp.dot(link_block.T, jnp.dot(neg_re, link_block, precision=LINK), precision=LINK)
            )
            next_im = -symmetric(
                jnp.dot(link_block.T, jnp.dot(neg_im, link_block, precision=LINK), precision=LINK)
            )
            left_re = jnp.where(is_left, next_re, left_re)
            left_im = jnp.where(is_left, next_im, left_im)
            keep_right = jnp.logical_or(is_left, is_final)
            right_re = jnp.where(keep_right, right_re, next_re)
            right_im = jnp.where(keep_right, right_im, next_im)
            return (left_re, left_im, right_re, right_im, neg_re, neg_im)

        carry = lax.fori_loop(0, slab_total, chain_step, (zero_block,) * 6)
        outputs.append(jnp.stack([carry[4], carry[5]]))
    return jnp.stack(outputs)[None]


def solution(mesh):
    in_specs = (
        P("dom", None, None),
        P("dom", None, None),
        P("dom", None),
        P("energy", "dom", None, None, None),
        P(),
        P(),
        P(),
    )
    out_specs = P("energy", "dom", None, None, None)
    return jax.shard_map(body, mesh=mesh, in_specs=in_specs, out_specs=out_specs, check_vma=False)
```
